512 devices in a mesh: act: 4 (over z_hi, core), axial: 16 (over x, y), hoop: 8 (over z_lo).
Axes of the slice: x: 4, y: 4, z: 16 (z_hi: 2, z_lo: 8; z = z_hi * 8 + z_lo), core: 2. Of those that a mesh axis runs over, the one named last changes fastest.
Arguments:
- wave_state: float32 [4, 5, 256, 4096], P('act', None, 'axial', 'hoop'), may hold values from -6 to 6
- layup_zone: int32 [256, 4096], P('axial', 'hoop'), may hold values from 0 to 7
- moduli: float32 [8, 6], replicated, may hold values from 0.1 to 0.35
- sensors: int32 [512], P(('axial', 'hoop')), may hold values from 0 to 8191
- history: float32 [4, 512, 253], P('act', ('axial', 'hoop')), may hold values from -6 to 6
- receivers: int32 [4, 128], P('act'), may hold values from 0 to 511, as said below
- delays: int32 [4, 128, 256, 1024], P('act', None, 'axial', 'hoop'), may hold values from 0 to 255
Outputs:
- next_state: float32 [4, 5, 256, 4096], P('act', None, 'axial', 'hoop')
- traces: float32 [4, 512, 3], P('act', ('axial', 'hoop'))
- damage_map: float32 [256, 1024], P('axial', 'hoop')
The draws below stay inside these ranges and needn't reach their ends.
Inputs may be any that keep to these rules, and one draw needn't show every extreme that they name: `receivers`: each row names 128 different sensors.
All inputs are finite; a program needn't handle non-finite values.
Results may differ from the reference program's by a relative error of at most 0.000029.
Values sent between devices are 32-bit elements; how exact they have to be, the bound alone decides.
No kernel may reach another device: no remote copies, remote signals or barrier semaphores. Data moves between devices by JAX's collectives and lax.ppermute only.
A program may use at most 64 MiB of HBM per device.

```python
import jax
import jax.numpy as jnp
from jax import lax

CA = 16
CH = 512
STEPS = 3
NT = 256
SENS_DEV = 4
LAYUPS = 8
HIST = 253
NA = 256
NH = 4096
ACTS = 4
SENSORS = 512
PAIRS = 128
NPA = 256
NPH = 1024
N_HOOP = 8


def draw_receivers(key, part):

    def one_row(row_key):
        inner = jax.random.permutation(row_key, SENSORS - 2)[:PAIRS - 2].astype(jnp.int32) + 1
        chosen = jnp.concatenate([inner, jnp.array([0, SENSORS - 1], jnp.int32)])
        return jax.random.permutation(jax.random.fold_in(row_key, 7), chosen)
    row_keys = jax.random.split(key, ACTS)
    return jax.vmap(one_row)(row_keys).astype(jnp.int32)


def place_ends(drawn, key, least, high):
    index_at = [jax.random.randint(jax.random.fold_in(key, axis), (), 0, length) for axis, length in enumerate(drawn.shape)]
    widest = drawn.shape.index(max(drawn.shape))
    beside = index_at[:widest] + [(index_at[widest] + 1) % drawn.shape[widest]] + index_at[widest + 1:]
    return drawn.at[tuple(index_at)].set(least).at[tuple(beside)].set(high)


def shard_levels(stream_key, shape, pieces, smallest, top_value):
    level, own = 1.0, jax.random.fold_in(stream_key, 6)
    for axis_at, shards_of in pieces:
        heights = jnp.exp(jax.random.uniform(jax.random.fold_in(own, axis_at), (shards_of,), jnp.float32, smallest / len(pieces), top_value / len(pieces)))
        level = level * jnp.repeat(heights, shape[axis_at] // shards_of).reshape([-1 if axis == axis_at else 1 for axis in range(len(shape))])
    return level


def centred(stream_key, extent, scale, reach, cuts=(), kind=jnp.bfloat16):
    result = scale * jax.random.normal(stream_key, extent, jnp.float32)
    if cuts:
        result = result * shard_levels(stream_key, extent, cuts, -0.22, 0.18)
    return jnp.clip(result, -reach, reach).astype(kind)


def setup_inputs(seed: int = 0) -> dict:
    arg_keys = jax.random.split(jax.random.key(seed), 8)
    return {
        "wave_state": centred(arg_keys[0], (ACTS, 5, NA, NH), 1.0, 6.0, ((0, 4), (2, 16), (3, 8)), jnp.float32),
        "layup_zone": place_ends(jax.random.randint(arg_keys[1], (NA, NH), 0, LAYUPS), jax.random.fold_in(arg_keys[1], 1), 0, LAYUPS - 1).astype(jnp.int32),
        "moduli": jnp.clip(jax.random.uniform(arg_keys[2], (LAYUPS, 6), jnp.float32, 0.1, 0.35), 0.1, 0.35),
        "sensors": place_ends(jax.random.randint(arg_keys[3], (SENSORS,), 0, CA * CH), jax.random.fold_in(arg_keys[3], 1), 0, (CA * CH) - 1).astype(jnp.int32),
        "history": centred(arg_keys[4], (ACTS, SENSORS, HIST), 1.0, 6.0, ((0, 4), (1, 128)), jnp.float32),
        "receivers": draw_receivers(jax.random.fold_in(arg_keys[7], 71), 0),
        "delays": place_ends(jax.random.randint(arg_keys[6], (ACTS, PAIRS, NPA, NPH), 0, NT), jax.random.fold_in(arg_keys[6], 1), 0, NT - 1).astype(jnp.int32),
    }


def upper_axial(field):
    return jnp.concatenate([field[1:], jnp.zeros_like(field[:1])], axis=0)


def lower_axial(field):
    return jnp.concatenate([jnp.zeros_like(field[:1]), field[:-1]], axis=0)


def upper_hoop(field):
    return jnp.roll(field, -1, axis=1)


def lower_hoop(field):
    return jnp.roll(field, 1, axis=1)


def advance(fields, moduli_map):
    speed_axial, speed_hoop, normal_axial, normal_hoop, shear_stress = fields
    mobility_axial, mobility_hoop, stiff_axial, stiff_cross, stiff_hoop, stiff_shear = moduli_map
    speed_axial = speed_axial + mobility_axial * ((upper_axial(normal_axial) - normal_axial) + (shear_stress - lower_hoop(shear_stress)))
    speed_hoop = speed_hoop + mobility_hoop * ((upper_hoop(normal_hoop) - normal_hoop) + (shear_stress - lower_axial(shear_stress)))
    strain_axial = speed_axial - lower_axial(speed_axial)
    strain_hoop = speed_hoop - lower_hoop(speed_hoop)
    normal_axial = normal_axial + stiff_axial * strain_axial + stiff_cross * strain_hoop
    normal_hoop = normal_hoop + stiff_cross * strain_axial + stiff_hoop * strain_hoop
    strain_shear = (upper_hoop(speed_axial) - speed_axial) + (upper_axial(speed_hoop) - speed_hoop)
    shear_stress = shear_stress + stiff_shear * strain_shear
    return (speed_axial, speed_hoop, normal_axial, normal_hoop, shear_stress)


def add_pair(running, pair_item):
    row_values, row_delays = pair_item
    return running + row_values[row_delays], None


def reference(wave_state, layup_zone, moduli, sensors, history, receivers, delays):
    moduli_map = jnp.moveaxis(moduli[layup_zone], 2, 0)
    sensor_ids = jnp.arange(SENSORS, dtype=jnp.int32)
    sensor_block = sensor_ids // SENS_DEV
    sensor_row = ((sensor_block // N_HOOP) * CA + sensors // CH).astype(jnp.int32)
    sensor_col = ((sensor_block % N_HOOP) * CH + sensors % CH).astype(jnp.int32)
    states = []
    recorded_all = []
    summed = jnp.zeros((NPA * NPH,), jnp.float32)
    for actuator in range(ACTS):
        fields = tuple(wave_state[actuator, component] for component in range(5))
        samples = []
        for step_index in range(STEPS):
            fields = advance(fields, moduli_map)
            samples.append((fields[2] + fields[3])[sensor_row, sensor_col])
        recorded = jnp.stack(samples, axis=1)
        states.append(jnp.stack(fields))
        recorded_all.append(recorded)
        waveforms = jnp.concatenate([history[actuator], recorded], axis=1)
        chosen_rows = waveforms[receivers[actuator]]
        flat_delays = delays[actuator].reshape(PAIRS, NPA * NPH)
        summed = lax.scan(add_pair, summed, (chosen_rows, flat_delays))[0]
    energy = summed * summed / (PAIRS * ACTS)
    return jnp.stack(states), jnp.stack(recorded_all), energy.reshape(NPA, NPH)
```

```python
import functools

import jax
import jax.numpy as jnp
from jax import lax
from jax.experimental import pallas as pl
from jax.experimental.pallas import tpu as pltpu
from jax.sharding import PartitionSpec as P

STEPS = 3
HALO = 2 * STEPS


def exchange(cells, halo):
    na = lax.axis_size("axial")
    nh = lax.axis_size("hoop")
    from_above = lax.ppermute(cells[:, -halo:, :], "axial", [(i, i + 1) for i in range(na - 1)])
    from_below = lax.ppermute(cells[:, :halo, :], "axial", [(i + 1, i) for i in range(na - 1)])
    cells = jnp.concatenate([from_above, cells, from_below], axis=1)
    from_left = lax.ppermute(cells[:, :, -halo:], "hoop", [(j, (j + 1) % nh) for j in range(nh)])
    from_right = lax.ppermute(cells[:, :, :halo], "hoop", [((j + 1) % nh, j) for j in range(nh)])
    return jnp.concatenate([from_left, cells, from_right], axis=2)


def inner(f):
    return f[1:-1, 1:-1]


def advance(fields, moduli_map):
    speed_axial, speed_hoop, normal_axial, normal_hoop, shear_stress = fields
    m = [inner(moduli_map[i]) for i in range(6)]
    mobility_axial, mobility_hoop = m[0], m[1]
    na_c = inner(normal_axial)
    nh_c = inner(normal_hoop)
    ss_c = inner(shear_stress)
    speed_axial = inner(speed_axial) + mobility_axial * (
        (normal_axial[2:, 1:-1] - na_c) + (ss_c - shear_stress[1:-1, :-2])
    )
    speed_hoop = inner(speed_hoop) + mobility_hoop * (
        (normal_hoop[1:-1, 2:] - nh_c) + (ss_c - shear_stress[:-2, 1:-1])
    )
    stiff_axial, stiff_cross, stiff_hoop, stiff_shear = (inner(m[i]) for i in range(2, 6))
    va_c = inner(speed_axial)
    vh_c = inner(speed_hoop)
    strain_axial = va_c - speed_axial[:-2, 1:-1]
    strain_hoop = vh_c - speed_hoop[1:-1, :-2]
    normal_axial = inner(na_c) + stiff_axial * strain_axial + stiff_cross * strain_hoop
    normal_hoop = inner(nh_c) + stiff_cross * strain_axial + stiff_hoop * strain_hoop
    strain_shear = (speed_axial[1:-1, 2:] - va_c) + (speed_hoop[2:, 1:-1] - vh_c)
    shear_stress = inner(ss_c) + stiff_shear * strain_shear
    return (va_c, vh_c, normal_axial, normal_hoop, shear_stress), m


def image_kernel(rows_ref, delays_ref, out_ref):
    pairs, pix_rows, pix_cols = delays_ref.shape
    lanes = rows_ref.shape[1]

    def body(k, acc):
        d = delays_ref[k]
        low = jnp.broadcast_to(rows_ref[pl.ds(2 * k, 1), :], (pix_rows, pix_cols))
        high = jnp.broadcast_to(rows_ref[pl.ds(2 * k + 1, 1), :], (pix_rows, pix_cols))
        idx = d & (lanes - 1)
        got_low = jnp.take_along_axis(low, idx, axis=1, mode="promise_in_bounds")
        got_high = jnp.take_along_axis(high, idx, axis=1, mode="promise_in_bounds")
        return acc + jnp.where(d >= lanes, got_high, got_low)

    acc = lax.fori_loop(0, pairs, body, jnp.zeros((pix_rows, pix_cols), jnp.float32), unroll=8)
    out_ref[...] = acc


def image(rows, delays):
    pairs, pix_rows, pix_cols = delays.shape
    return pl.pallas_call(
        image_kernel,
        out_shape=jax.ShapeDtypeStruct((pix_rows, pix_cols), jnp.float32),
        in_specs=[pl.BlockSpec(memory_space=pltpu.VMEM)] * 2,
        out_specs=pl.BlockSpec(memory_space=pltpu.VMEM),
        cost_estimate=pl.CostEstimate(
            flops=8 * pairs * pix_rows * pix_cols,
            bytes_accessed=4 * (rows.size + delays.size + pix_rows * pix_cols),
            transcendentals=0,
        ),
    )(rows, delays)


def gather_waves(local_waves):
    inner_waves = lax.all_gather(local_waves, "hoop", axis=0, tiled=True)
    return lax.all_gather(inner_waves, "axial", axis=0, tiled=True)


def per_device(wave_state, layup_zone, moduli, sensors, history, receivers, delays):
    rows, cols = layup_zone.shape
    na = lax.axis_size("axial")
    stacked = jnp.concatenate(
        [wave_state[0], layup_zone.astype(jnp.float32)[None]], axis=0
    )
    padded = exchange(stacked, HALO)
    zone = padded[5].astype(jnp.int32)
    global_row = lax.axis_index("axial") * rows - HALO + lax.broadcasted_iota(
        jnp.int32, zone.shape, 0
    )
    inside = (global_row >= 0) & (global_row < na * rows)
    moduli_map = jnp.zeros((moduli.shape[1],) + zone.shape, jnp.float32)
    for zone_level in range(moduli.shape[0]):
        moduli_map = jnp.where(
            (zone == zone_level)[None], moduli[zone_level][:, None, None], moduli_map
        )
    moduli_map = jnp.where(inside[None], moduli_map, jnp.float32(0.0))
    fields = tuple(padded[c] for c in range(5))
    samples = []
    for step_index in range(STEPS):
        fields, moduli_map = advance(fields, moduli_map)
        moduli_map = [inner(m) for m in moduli_map]
        off = HALO - 2 * (step_index + 1)
        total = fields[2] + fields[3]
        tile = total[off:off + rows, off:off + cols]
        samples.append(tile.reshape(-1)[sensors])
        moduli_map = jnp.stack(moduli_map)
    next_state = jnp.stack(fields)[None]
    recorded = jnp.stack(samples, axis=1)[None]
    local_waves = jnp.concatenate([history[0], recorded[0]], axis=1)
    waveforms = gather_waves(local_waves)
    sample_count = waveforms.shape[1]
    chosen = waveforms[receivers[0]].reshape(2 * receivers.shape[1], sample_count // 2)
    partial_value = image(chosen, delays[0])
    summed = lax.psum(partial_value, "act")
    damage_map = summed * summed / (receivers.shape[1] * lax.axis_size("act"))
    return (next_state, recorded, damage_map)


def solution(mesh):
    return jax.shard_map(
        per_device,
        mesh=mesh,
        in_specs=(
            P("act", None, "axial", "hoop"),
            P("axial", "hoop"),
            P(),
            P(("axial", "hoop")),
            P("act", ("axial", "hoop"), None),
            P("act", None),
            P("act", None, "axial", "hoop"),
        ),
        out_specs=(
            P("act", None, "axial", "hoop"),
            P("act", ("axial", "hoop"), None),
            P("axial", "hoop"),
        ),
        check_vma=False,
    )
```

```python
import functools

import jax
import jax.numpy as jnp
from jax import lax
from jax.experimental import pallas as pl
from jax.experimental.pallas import tpu as pltpu
from jax.sharding import PartitionSpec as P

STEPS = 3
HALO = 2 * STEPS


def exchange(cells, halo):
    na = lax.axis_size("axial")
    nh = lax.axis_size("hoop")
    from_above = lax.ppermute(cells[:, -halo:, :], "axial", [(i, i + 1) for i in range(na - 1)])
    from_below = lax.ppermute(cells[:, :halo, :], "axial", [(i + 1, i) for i in range(na - 1)])
    cells = jnp.concatenate([from_above, cells, from_below], axis=1)
    from_left = lax.ppermute(cells[:, :, -halo:], "hoop", [(j, (j + 1) % nh) for j in range(nh)])
    from_right = lax.ppermute(cells[:, :, :halo], "hoop", [((j + 1) % nh, j) for j in range(nh)])
    return jnp.concatenate([from_left, cells, from_right], axis=2)


def inner(f):
    return f[1:-1, 1:-1]


def advance(fields, moduli_map):
    speed_axial, speed_hoop, normal_axial, normal_hoop, shear_stress = fields
    m = [inner(moduli_map[i]) for i in range(6)]
    mobility_axial, mobility_hoop = m[0], m[1]
    na_c = inner(normal_axial)
    nh_c = inner(normal_hoop)
    ss_c = inner(shear_stress)
    speed_axial = inner(speed_axial) + mobility_axial * (
        (normal_axial[2:, 1:-1] - na_c) + (ss_c - shear_stress[1:-1, :-2])
    )
    speed_hoop = inner(speed_hoop) + mobility_hoop * (
        (normal_hoop[1:-1, 2:] - nh_c) + (ss_c - shear_stress[:-2, 1:-1])
    )
    stiff_axial, stiff_cross, stiff_hoop, stiff_shear = (inner(m[i]) for i in range(2, 6))
    va_c = inner(speed_axial)
    vh_c = inner(speed_hoop)
    strain_axial = va_c - speed_axial[:-2, 1:-1]
    strain_hoop = vh_c - speed_hoop[1:-1, :-2]
    normal_axial = inner(na_c) + stiff_axial * strain_axial + stiff_cross * strain_hoop
    normal_hoop = inner(nh_c) + stiff_cross * strain_axial + stiff_hoop * strain_hoop
    strain_shear = (speed_axial[1:-1, 2:] - va_c) + (speed_hoop[2:, 1:-1] - vh_c)
    shear_stress = inner(ss_c) + stiff_shear * strain_shear
    return (va_c, vh_c, normal_axial, normal_hoop, shear_stress), m


def image_kernel(rows_ref, delays_ref, out_ref):
    pairs, pix_rows, pix_cols = delays_ref.shape
    lanes = rows_ref.shape[1]

    def body(k, acc):
        d = delays_ref[k]
        low = jnp.broadcast_to(rows_ref[pl.ds(2 * k, 1), :], (pix_rows, pix_cols))
        high = jnp.broadcast_to(rows_ref[pl.ds(2 * k + 1, 1), :], (pix_rows, pix_cols))
        idx = d & (lanes - 1)
        got_low = jnp.take_along_axis(low, idx, axis=1, mode="promise_in_bounds")
        got_high = jnp.take_along_axis(high, idx, axis=1, mode="promise_in_bounds")
        return acc + jnp.where(d >= lanes, got_high, got_low)

    acc = lax.fori_loop(0, pairs, body, jnp.zeros((pix_rows, pix_cols), jnp.float32), unroll=8)
    out_ref[...] = acc


def image(rows, delays):
    pairs, pix_rows, pix_cols = delays.shape
    return pl.pallas_call(
        image_kernel,
        out_shape=jax.ShapeDtypeStruct((pix_rows, pix_cols), jnp.float32),
        in_specs=[pl.BlockSpec(memory_space=pltpu.VMEM)] * 2,
        out_specs=pl.BlockSpec(memory_space=pltpu.VMEM),
        cost_estimate=pl.CostEstimate(
            flops=8 * pairs * pix_rows * pix_cols,
            bytes_accessed=4 * (rows.size + delays.size + pix_rows * pix_cols),
            transcendentals=0,
        ),
    )(rows, delays)


def gather_doubling(block, axis):
    count = lax.axis_size(axis)
    me = lax.axis_index(axis)
    stride = 1
    while stride < count:
        other = lax.ppermute(block, axis, [(i, i ^ stride) for i in range(count)])
        lower = (me // stride) % 2 == 0
        block = jnp.where(
            lower, jnp.concatenate([block, other]), jnp.concatenate([other, block])
        )
        stride *= 2
    return block


def gather_waves(local_waves):
    return gather_doubling(gather_doubling(local_waves, "hoop"), "axial")


def per_device(wave_state, layup_zone, moduli, sensors, history, receivers, delays):
    rows, cols = layup_zone.shape
    na = lax.axis_size("axial")
    stacked = jnp.concatenate(
        [wave_state[0], layup_zone.astype(jnp.float32)[None]], axis=0
    )
    padded = exchange(stacked, HALO)
    zone = padded[5].astype(jnp.int32)
    global_row = lax.axis_index("axial") * rows - HALO + lax.broadcasted_iota(
        jnp.int32, zone.shape, 0
    )
    inside = (global_row >= 0) & (global_row < na * rows)
    moduli_map = jnp.zeros((moduli.shape[1],) + zone.shape, jnp.float32)
    for zone_level in range(moduli.shape[0]):
        moduli_map = jnp.where(
            (zone == zone_level)[None], moduli[zone_level][:, None, None], moduli_map
        )
    moduli_map = jnp.where(inside[None], moduli_map, jnp.float32(0.0))
    fields = tuple(padded[c] for c in range(5))
    samples = []
    for step_index in range(STEPS):
        fields, moduli_map = advance(fields, moduli_map)
        moduli_map = [inner(m) for m in moduli_map]
        off = HALO - 2 * (step_index + 1)
        total = fields[2] + fields[3]
        tile = total[off:off + rows, off:off + cols]
        samples.append(tile.reshape(-1)[sensors])
        moduli_map = jnp.stack(moduli_map)
    next_state = jnp.stack(fields)[None]
    recorded = jnp.stack(samples, axis=1)[None]
    local_waves = jnp.concatenate([history[0], recorded[0]], axis=1)
    waveforms = gather_waves(local_waves)
    sample_count = waveforms.shape[1]
    chosen = waveforms[receivers[0]].reshape(2 * receivers.shape[1], sample_count // 2)
    partial_value = image(chosen, delays[0])
    summed = lax.psum(partial_value, "act")
    damage_map = summed * summed / (receivers.shape[1] * lax.axis_size("act"))
    return (next_state, recorded, damage_map)


def solution(mesh):
    return jax.shard_map(
        per_device,
        mesh=mesh,
        in_specs=(
            P("act", None, "axial", "hoop"),
            P("axial", "hoop"),
            P(),
            P(("axial", "hoop")),
            P("act", ("axial", "hoop"), None),
            P("act", None),
            P("act", None, "axial", "hoop"),
        ),
        out_specs=(
            P("act", None, "axial", "hoop"),
            P("act", ("axial", "hoop"), None),
            P("axial", "hoop"),
        ),
        check_vma=False,
    )
```

```python
import functools

import jax
import jax.numpy as jnp
from jax import lax
from jax.experimental import pallas as pl
from jax.experimental.pallas import tpu as pltpu
from jax.sharding import PartitionSpec as P

STEPS = 3
HALO = 2 * STEPS


def exchange(cells, halo):
    na = lax.axis_size("axial")
    nh = lax.axis_size("hoop")
    from_above = lax.ppermute(cells[:, -halo:, :], "axial", [(i, i + 1) for i in range(na - 1)])
    from_below = lax.ppermute(cells[:, :halo, :], "axial", [(i + 1, i) for i in range(na - 1)])
    cells = jnp.concatenate([from_above, cells, from_below], axis=1)
    from_left = lax.ppermute(cells[:, :, -halo:], "hoop", [(j, (j + 1) % nh) for j in range(nh)])
    from_right = lax.ppermute(cells[:, :, :halo], "hoop", [((j + 1) % nh, j) for j in range(nh)])
    return jnp.concatenate([from_left, cells, from_right], axis=2)


def inner(f):
    return f[1:-1, 1:-1]


def advance(fields, moduli_map):
    speed_axial, speed_hoop, normal_axial, normal_hoop, shear_stress = fields
    m = [inner(moduli_map[i]) for i in range(6)]
    mobility_axial, mobility_hoop = m[0], m[1]
    na_c = inner(normal_axial)
    nh_c = inner(normal_hoop)
    ss_c = inner(shear_stress)
    speed_axial = inner(speed_axial) + mobility_axial * (
        (normal_axial[2:, 1:-1] - na_c) + (ss_c - shear_stress[1:-1, :-2])
    )
    speed_hoop = inner(speed_hoop) + mobility_hoop * (
        (normal_hoop[1:-1, 2:] - nh_c) + (ss_c - shear_stress[:-2, 1:-1])
    )
    stiff_axial, stiff_cross, stiff_hoop, stiff_shear = (inner(m[i]) for i in range(2, 6))
    va_c = inner(speed_axial)
    vh_c = inner(speed_hoop)
    strain_axial = va_c - speed_axial[:-2, 1:-1]
    strain_hoop = vh_c - speed_hoop[1:-1, :-2]
    normal_axial = inner(na_c) + stiff_axial * strain_axial + stiff_cross * strain_hoop
    normal_hoop = inner(nh_c) + stiff_cross * strain_axial + stiff_hoop * strain_hoop
    strain_shear = (speed_axial[1:-1, 2:] - va_c) + (speed_hoop[2:, 1:-1] - vh_c)
    shear_stress = inner(ss_c) + stiff_shear * strain_shear
    return (va_c, vh_c, normal_axial, normal_hoop, shear_stress), m


def image_kernel(rows_ref, delays_ref, out_ref):
    pairs, pix_rows, pix_cols = delays_ref.shape
    lanes = rows_ref.shape[1]

    def body(k, acc):
        d = delays_ref[k]
        low = jnp.broadcast_to(rows_ref[pl.ds(2 * k, 1), :], (pix_rows, pix_cols))
        high = jnp.broadcast_to(rows_ref[pl.ds(2 * k + 1, 1), :], (pix_rows, pix_cols))
        idx = d & (lanes - 1)
        got_low = jnp.take_along_axis(low, idx, axis=1, mode="promise_in_bounds")
        got_high = jnp.take_along_axis(high, idx, axis=1, mode="promise_in_bounds")
        return acc + jnp.where(d >= lanes, got_high, got_low)

    acc = lax.fori_loop(0, pairs, body, jnp.zeros((pix_rows, pix_cols), jnp.float32), unroll=8)
    out_ref[...] = acc


def image(rows, delays):
    pairs, pix_rows, pix_cols = delays.shape
    return pl.pallas_call(
        image_kernel,
        out_shape=jax.ShapeDtypeStruct((pix_rows, pix_cols), jnp.float32),
        in_specs=[pl.BlockSpec(memory_space=pltpu.VMEM)] * 2,
        out_specs=pl.BlockSpec(memory_space=pltpu.VMEM),
        cost_estimate=pl.CostEstimate(
            flops=8 * pairs * pix_rows * pix_cols,
            bytes_accessed=4 * (rows.size + delays.size + pix_rows * pix_cols),
            transcendentals=0,
        ),
    )(rows, delays)


def trace_kernel(first, samples, tr_ref, delays_ref, acc_ref, out_ref):
    pairs = delays_ref.shape[0]

    def body(k, acc):
        d = delays_ref[k]
        add = jnp.zeros_like(acc)
        for t in range(samples - 1, -1, -1):
            add = jnp.where(d == first + t, tr_ref[samples * k + t], add)
        return acc + add

    out_ref[...] = lax.fori_loop(0, pairs, body, acc_ref[...], unroll=8)


def add_traces(first, tr, delays, acc):
    pairs, pix_rows, pix_cols = delays.shape
    samples = tr.shape[1]
    return pl.pallas_call(
        functools.partial(trace_kernel, first, samples),
        out_shape=jax.ShapeDtypeStruct((pix_rows, pix_cols), jnp.float32),
        in_specs=[
            pl.BlockSpec(memory_space=pltpu.SMEM),
            pl.BlockSpec(memory_space=pltpu.VMEM),
            pl.BlockSpec(memory_space=pltpu.VMEM),
        ],
        out_specs=pl.BlockSpec(memory_space=pltpu.VMEM),
        cost_estimate=pl.CostEstimate(
            flops=7 * pairs * pix_rows * pix_cols,
            bytes_accessed=4 * (delays.size + 2 * pix_rows * pix_cols),
            transcendentals=0,
        ),
    )(tr.reshape(-1), delays, acc)


def gather_doubling(block, axis):
    count = lax.axis_size(axis)
    me = lax.axis_index(axis)
    stride = 1
    while stride < count:
        other = lax.ppermute(block, axis, [(i, i ^ stride) for i in range(count)])
        lower = (me // stride) % 2 == 0
        block = jnp.where(
            lower, jnp.concatenate([block, other]), jnp.concatenate([other, block])
        )
        stride *= 2
    return block


def gather_waves(local_waves):
    return gather_doubling(gather_doubling(local_waves, "hoop"), "axial")


def per_device(wave_state, layup_zone, moduli, sensors, history, receivers, delays):
    rows, cols = layup_zone.shape
    na = lax.axis_size("axial")
    stacked = jnp.concatenate(
        [wave_state[0], layup_zone.astype(jnp.float32)[None]], axis=0
    )
    padded = exchange(stacked, HALO)
    zone = padded[5].astype(jnp.int32)
    global_row = lax.axis_index("axial") * rows - HALO + lax.broadcasted_iota(
        jnp.int32, zone.shape, 0
    )
    inside = (global_row >= 0) & (global_row < na * rows)
    moduli_map = jnp.zeros((moduli.shape[1],) + zone.shape, jnp.float32)
    for zone_level in range(moduli.shape[0]):
        moduli_map = jnp.where(
            (zone == zone_level)[None], moduli[zone_level][:, None, None], moduli_map
        )
    moduli_map = jnp.where(inside[None], moduli_map, jnp.float32(0.0))
    fields = tuple(padded[c] for c in range(5))
    samples = []
    for step_index in range(STEPS):
        fields, moduli_map = advance(fields, moduli_map)
        moduli_map = [inner(m) for m in moduli_map]
        off = HALO - 2 * (step_index + 1)
        total = fields[2] + fields[3]
        tile = total[off:off + rows, off:off + cols]
        samples.append(tile.reshape(-1)[sensors])
        moduli_map = jnp.stack(moduli_map)
    next_state = jnp.stack(fields)[None]
    recorded = jnp.stack(samples, axis=1)[None]
    hist = history[0]
    hist_count = hist.shape[1]
    sample_count = hist_count + STEPS
    padded_hist = jnp.concatenate(
        [hist, jnp.zeros((hist.shape[0], sample_count - hist_count), jnp.float32)], axis=1
    )
    all_hist = gather_waves(padded_hist)
    all_traces = gather_waves(recorded[0])
    chosen = all_hist[receivers[0]].reshape(2 * receivers.shape[1], sample_count // 2)
    partial_value = image(chosen, delays[0])
    partial_value = add_traces(hist_count, all_traces[receivers[0]], delays[0], partial_value)
    summed = lax.psum(partial_value, "act")
    damage_map = summed * summed / (receivers.shape[1] * lax.axis_size("act"))
    return (next_state, recorded, damage_map)


def solution(mesh):
    return jax.shard_map(
        per_device,
        mesh=mesh,
        in_specs=(
            P("act", None, "axial", "hoop"),
            P("axial", "hoop"),
            P(),
            P(("axial", "hoop")),
            P("act", ("axial", "hoop"), None),
            P("act", None),
            P("act", None, "axial", "hoop"),
        ),
        out_specs=(
            P("act", None, "axial", "hoop"),
            P("act", ("axial", "hoop"), None),
            P("axial", "hoop"),
        ),
        check_vma=False,
    )
```

```python
import functools

import jax
import jax.numpy as jnp
from jax import lax
from jax.experimental import pallas as pl
from jax.experimental.pallas import tpu as pltpu
from jax.sharding import PartitionSpec as P

STEPS = 3
HALO = 2 * STEPS


def exchange(cells, halo):
    na = lax.axis_size("axial")
    nh = lax.axis_size("hoop")
    from_above = lax.ppermute(cells[:, -halo:, :], "axial", [(i, i + 1) for i in range(na - 1)])
    from_below = lax.ppermute(cells[:, :halo, :], "axial", [(i + 1, i) for i in range(na - 1)])
    cells = jnp.concatenate([from_above, cells, from_below], axis=1)
    from_left = lax.ppermute(cells[:, :, -halo:], "hoop", [(j, (j + 1) % nh) for j in range(nh)])
    from_right = lax.ppermute(cells[:, :, :halo], "hoop", [((j + 1) % nh, j) for j in range(nh)])
    return jnp.concatenate([from_left, cells, from_right], axis=2)


def inner(f):
    return f[1:-1, 1:-1]


def advance(fields, moduli_map):
    speed_axial, speed_hoop, normal_axial, normal_hoop, shear_stress = fields
    m = [inner(moduli_map[i]) for i in range(6)]
    mobility_axial, mobility_hoop = m[0], m[1]
    na_c = inner(normal_axial)
    nh_c = inner(normal_hoop)
    ss_c = inner(shear_stress)
    speed_axial = inner(speed_axial) + mobility_axial * (
        (normal_axial[2:, 1:-1] - na_c) + (ss_c - shear_stress[1:-1, :-2])
    )
    speed_hoop = inner(speed_hoop) + mobility_hoop * (
        (normal_hoop[1:-1, 2:] - nh_c) + (ss_c - shear_stress[:-2, 1:-1])
    )
    stiff_axial, stiff_cross, stiff_hoop, stiff_shear = (inner(m[i]) for i in range(2, 6))
    va_c = inner(speed_axial)
    vh_c = inner(speed_hoop)
    strain_axial = va_c - speed_axial[:-2, 1:-1]
    strain_hoop = vh_c - speed_hoop[1:-1, :-2]
    normal_axial = inner(na_c) + stiff_axial * strain_axial + stiff_cross * strain_hoop
    normal_hoop = inner(nh_c) + stiff_cross * strain_axial + stiff_hoop * strain_hoop
    strain_shear = (speed_axial[1:-1, 2:] - va_c) + (speed_hoop[2:, 1:-1] - vh_c)
    shear_stress = inner(ss_c) + stiff_shear * strain_shear
    return (va_c, vh_c, normal_axial, normal_hoop, shear_stress), m


def image_kernel(rows_ref, delays_ref, out_ref):
    pairs, pix_rows, pix_cols = delays_ref.shape
    lanes = rows_ref.shape[1]

    def body(k, acc):
        d = delays_ref[k]
        low = jnp.broadcast_to(rows_ref[pl.ds(2 * k, 1), :], (pix_rows, pix_cols))
        high = jnp.broadcast_to(rows_ref[pl.ds(2 * k + 1, 1), :], (pix_rows, pix_cols))
        idx = d & (lanes - 1)
        got_low = jnp.take_along_axis(low, idx, axis=1, mode="promise_in_bounds")
        got_high = jnp.take_along_axis(high, idx, axis=1, mode="promise_in_bounds")
        return acc + jnp.where(d >= lanes, got_high, got_low)

    acc = lax.fori_loop(0, pairs, body, jnp.zeros((pix_rows, pix_cols), jnp.float32), unroll=8)
    out_ref[...] = acc


def image(rows, delays):
    pairs, pix_rows, pix_cols = delays.shape
    return pl.pallas_call(
        image_kernel,
        out_shape=jax.ShapeDtypeStruct((pix_rows, pix_cols), jnp.float32),
        in_specs=[pl.BlockSpec(memory_space=pltpu.VMEM)] * 2,
        out_specs=pl.BlockSpec(memory_space=pltpu.VMEM),
        cost_estimate=pl.CostEstimate(
            flops=8 * pairs * pix_rows * pix_cols,
            bytes_accessed=4 * (rows.size + delays.size + pix_rows * pix_cols),
            transcendentals=0,
        ),
    )(rows, delays)


def gather_doubling(block, axis):
    count = lax.axis_size(axis)
    me = lax.axis_index(axis)
    stride = 1
    while stride < count:
        other = lax.ppermute(block, axis, [(i, i ^ stride) for i in range(count)])
        lower = (me // stride) % 2 == 0
        block = jnp.where(
            lower, jnp.concatenate([block, other]), jnp.concatenate([other, block])
        )
        stride *= 2
    return block


def gather_waves(local_waves):
    return gather_doubling(gather_doubling(local_waves, "hoop"), "axial")


def act_sum(partial_value):
    count = lax.axis_size("act")
    stride = 1
    while stride < count:
        partial_value = partial_value + lax.ppermute(
            partial_value, "act", [(i, i ^ stride) for i in range(count)]
        )
        stride *= 2
    return partial_value


def per_device(wave_state, layup_zone, moduli, sensors, history, receivers, delays):
    rows, cols = layup_zone.shape
    na = lax.axis_size("axial")
    stacked = jnp.concatenate(
        [wave_state[0], layup_zone.astype(jnp.float32)[None]], axis=0
    )
    padded = exchange(stacked, HALO)
    zone = padded[5].astype(jnp.int32)
    global_row = lax.axis_index("axial") * rows - HALO + lax.broadcasted_iota(
        jnp.int32, zone.shape, 0
    )
    inside = (global_row >= 0) & (global_row < na * rows)
    moduli_map = jnp.zeros((moduli.shape[1],) + zone.shape, jnp.float32)
    for zone_level in range(moduli.shape[0]):
        moduli_map = jnp.where(
            (zone == zone_level)[None], moduli[zone_level][:, None, None], moduli_map
        )
    moduli_map = jnp.where(inside[None], moduli_map, jnp.float32(0.0))
    fields = tuple(padded[c] for c in range(5))
    samples = []
    for step_index in range(STEPS):
        fields, moduli_map = advance(fields, moduli_map)
        moduli_map = [inner(m) for m in moduli_map]
        off = HALO - 2 * (step_index + 1)
        total = fields[2] + fields[3]
        tile = total[off:off + rows, off:off + cols]
        samples.append(tile.reshape(-1)[sensors])
        moduli_map = jnp.stack(moduli_map)
    next_state = jnp.stack(fields)[None]
    recorded = jnp.stack(samples, axis=1)[None]
    local_waves = jnp.concatenate([history[0], recorded[0]], axis=1)
    waveforms = gather_waves(local_waves)
    sample_count = waveforms.shape[1]
    chosen = waveforms[receivers[0]].reshape(2 * receivers.shape[1], sample_count // 2)
    partial_value = image(chosen, delays[0])
    summed = act_sum(partial_value)
    damage_map = summed * summed / (receivers.shape[1] * lax.axis_size("act"))
    return (next_state, recorded, damage_map)


def solution(mesh):
    return jax.shard_map(
        per_device,
        mesh=mesh,
        in_specs=(
            P("act", None, "axial", "hoop"),
            P("axial", "hoop"),
            P(),
            P(("axial", "hoop")),
            P("act", ("axial", "hoop"), None),
            P("act", None),
            P("act", None, "axial", "hoop"),
        ),
        out_specs=(
            P("act", None, "axial", "hoop"),
            P("act", ("axial", "hoop"), None),
            P("axial", "hoop"),
        ),
        check_vma=False,
    )
```

```python
import functools

import jax
import jax.numpy as jnp
from jax import lax
from jax.experimental import pallas as pl
from jax.experimental.pallas import tpu as pltpu
from jax.sharding import PartitionSpec as P

STEPS = 3
HALO = 2 * STEPS


def exchange(cells, halo):
    na = lax.axis_size("axial")
    nh = lax.axis_size("hoop")
    from_above = lax.ppermute(cells[:, -halo:, :], "axial", [(i, i + 1) for i in range(na - 1)])
    from_below = lax.ppermute(cells[:, :halo, :], "axial", [(i + 1, i) for i in range(na - 1)])
    cells = jnp.concatenate([from_above, cells, from_below], axis=1)
    from_left = lax.ppermute(cells[:, :, -halo:], "hoop", [(j, (j + 1) % nh) for j in range(nh)])
    from_right = lax.ppermute(cells[:, :, :halo], "hoop", [((j + 1) % nh, j) for j in range(nh)])
    return jnp.concatenate([from_left, cells, from_right], axis=2)


def inner(f):
    return f[1:-1, 1:-1]


def advance(fields, moduli_map):
    speed_axial, speed_hoop, normal_axial, normal_hoop, shear_stress = fields
    m = [inner(moduli_map[i]) for i in range(6)]
    mobility_axial, mobility_hoop = m[0], m[1]
    na_c = inner(normal_axial)
    nh_c = inner(normal_hoop)
    ss_c = inner(shear_stress)
    speed_axial = inner(speed_axial) + mobility_axial * (
        (normal_axial[2:, 1:-1] - na_c) + (ss_c - shear_stress[1:-1, :-2])
    )
    speed_hoop = inner(speed_hoop) + mobility_hoop * (
        (normal_hoop[1:-1, 2:] - nh_c) + (ss_c - shear_stress[:-2, 1:-1])
    )
    stiff_axial, stiff_cross, stiff_hoop, stiff_shear = (inner(m[i]) for i in range(2, 6))
    va_c = inner(speed_axial)
    vh_c = inner(speed_hoop)
    strain_axial = va_c - speed_axial[:-2, 1:-1]
    strain_hoop = vh_c - speed_hoop[1:-1, :-2]
    normal_axial = inner(na_c) + stiff_axial * strain_axial + stiff_cross * strain_hoop
    normal_hoop = inner(nh_c) + stiff_cross * strain_axial + stiff_hoop * strain_hoop
    strain_shear = (speed_axial[1:-1, 2:] - va_c) + (speed_hoop[2:, 1:-1] - vh_c)
    shear_stress = inner(ss_c) + stiff_shear * strain_shear
    return (va_c, vh_c, normal_axial, normal_hoop, shear_stress), m


def image_kernel(rows_ref, delays_ref, out_ref):
    pairs, pix_rows, pix_cols = delays_ref.shape
    lanes = rows_ref.shape[1]

    def body(k, acc):
        d = delays_ref[k]
        low = jnp.broadcast_to(rows_ref[pl.ds(2 * k, 1), :], (pix_rows, pix_cols))
        high = jnp.broadcast_to(rows_ref[pl.ds(2 * k + 1, 1), :], (pix_rows, pix_cols))
        idx = d & (lanes - 1)
        got_low = jnp.take_along_axis(low, idx, axis=1, mode="promise_in_bounds")
        got_high = jnp.take_along_axis(high, idx, axis=1, mode="promise_in_bounds")
        return acc + jnp.where(d >= lanes, got_high, got_low)

    acc = lax.fori_loop(0, pairs, body, jnp.zeros((pix_rows, pix_cols), jnp.float32), unroll=8)
    out_ref[...] = acc


def image(rows, delays):
    pairs, pix_rows, pix_cols = delays.shape
    return pl.pallas_call(
        image_kernel,
        out_shape=jax.ShapeDtypeStruct((pix_rows, pix_cols), jnp.float32),
        in_specs=[pl.BlockSpec(memory_space=pltpu.VMEM)] * 2,
        out_specs=pl.BlockSpec(memory_space=pltpu.VMEM),
        cost_estimate=pl.CostEstimate(
            flops=8 * pairs * pix_rows * pix_cols,
            bytes_accessed=4 * (rows.size + delays.size + pix_rows * pix_cols),
            transcendentals=0,
        ),
    )(rows, delays)


def gather_radix(block, axis, radix):
    count = lax.axis_size(axis)
    me = lax.axis_index(axis)
    stride = 1
    while stride < count:
        width = min(radix, count // stride)
        digit = (me // stride) % width
        received = [block]
        for shift in range(1, width):
            pairs = []
            for i in range(count):
                own = (i // stride) % width
                pairs.append((i, i + ((own + shift) % width - own) * stride))
            received.append(lax.ppermute(block, axis, pairs))
        order = (digit - jnp.arange(width, dtype=jnp.int32)) % width
        block = jnp.stack(received)[order].reshape((-1,) + block.shape[1:])
        stride *= width
    return block


def gather_waves(local_waves):
    return gather_radix(gather_radix(local_waves, "hoop", 4), "axial", 4)


def per_device(wave_state, layup_zone, moduli, sensors, history, receivers, delays):
    rows, cols = layup_zone.shape
    na = lax.axis_size("axial")
    stacked = jnp.concatenate(
        [wave_state[0], layup_zone.astype(jnp.float32)[None]], axis=0
    )
    padded = exchange(stacked, HALO)
    zone = padded[5].astype(jnp.int32)
    global_row = lax.axis_index("axial") * rows - HALO + lax.broadcasted_iota(
        jnp.int32, zone.shape, 0
    )
    inside = (global_row >= 0) & (global_row < na * rows)
    moduli_map = jnp.zeros((moduli.shape[1],) + zone.shape, jnp.float32)
    for zone_level in range(moduli.shape[0]):
        moduli_map = jnp.where(
            (zone == zone_level)[None], moduli[zone_level][:, None, None], moduli_map
        )
    moduli_map = jnp.where(inside[None], moduli_map, jnp.float32(0.0))
    fields = tuple(padded[c] for c in range(5))
    samples = []
    for step_index in range(STEPS):
        fields, moduli_map = advance(fields, moduli_map)
        moduli_map = [inner(m) for m in moduli_map]
        off = HALO - 2 * (step_index + 1)
        total = fields[2] + fields[3]
        tile = total[off:off + rows, off:off + cols]
        samples.append(tile.reshape(-1)[sensors])
        moduli_map = jnp.stack(moduli_map)
    next_state = jnp.stack(fields)[None]
    recorded = jnp.stack(samples, axis=1)[None]
    local_waves = jnp.concatenate([history[0], recorded[0]], axis=1)
    waveforms = gather_waves(local_waves)
    sample_count = waveforms.shape[1]
    chosen = waveforms[receivers[0]].reshape(2 * receivers.shape[1], sample_count // 2)
    partial_value = image(chosen, delays[0])
    summed = lax.psum(partial_value, "act")
    damage_map = summed * summed / (receivers.shape[1] * lax.axis_size("act"))
    return (next_state, recorded, damage_map)


def solution(mesh):
    return jax.shard_map(
        per_device,
        mesh=mesh,
        in_specs=(
            P("act", None, "axial", "hoop"),
            P("axial", "hoop"),
            P(),
            P(("axial", "hoop")),
            P("act", ("axial", "hoop"), None),
            P("act", None),
            P("act", None, "axial", "hoop"),
        ),
        out_specs=(
            P("act", None, "axial", "hoop"),
            P("act", ("axial", "hoop"), None),
            P("axial", "hoop"),
        ),
        check_vma=False,
    )
```

```python
import functools

import jax
import jax.numpy as jnp
from jax import lax
from jax.experimental import pallas as pl
from jax.experimental.pallas import tpu as pltpu
from jax.sharding import PartitionSpec as P

STEPS = 3
HALO = 2 * STEPS


def exchange(cells, halo):
    na = lax.axis_size("axial")
    nh = lax.axis_size("hoop")
    from_above = lax.ppermute(cells[:, -halo:, :], "axial", [(i, i + 1) for i in range(na - 1)])
    from_below = lax.ppermute(cells[:, :halo, :], "axial", [(i + 1, i) for i in range(na - 1)])
    cells = jnp.concatenate([from_above, cells, from_below], axis=1)
    from_left = lax.ppermute(cells[:, :, -halo:], "hoop", [(j, (j + 1) % nh) for j in range(nh)])
    from_right = lax.ppermute(cells[:, :, :halo], "hoop", [((j + 1) % nh, j) for j in range(nh)])
    return jnp.concatenate([from_left, cells, from_right], axis=2)


def inner(f):
    return f[1:-1, 1:-1]


def advance(fields, moduli_map):
    speed_axial, speed_hoop, normal_axial, normal_hoop, shear_stress = fields
    m = [inner(moduli_map[i]) for i in range(6)]
    mobility_axial, mobility_hoop = m[0], m[1]
    na_c = inner(normal_axial)
    nh_c = inner(normal_hoop)
    ss_c = inner(shear_stress)
    speed_axial = inner(speed_axial) + mobility_axial * (
        (normal_axial[2:, 1:-1] - na_c) + (ss_c - shear_stress[1:-1, :-2])
    )
    speed_hoop = inner(speed_hoop) + mobility_hoop * (
        (normal_hoop[1:-1, 2:] - nh_c) + (ss_c - shear_stress[:-2, 1:-1])
    )
    stiff_axial, stiff_cross, stiff_hoop, stiff_shear = (inner(m[i]) for i in range(2, 6))
    va_c = inner(speed_axial)
    vh_c = inner(speed_hoop)
    strain_axial = va_c - speed_axial[:-2, 1:-1]
    strain_hoop = vh_c - speed_hoop[1:-1, :-2]
    normal_axial = inner(na_c) + stiff_axial * strain_axial + stiff_cross * strain_hoop
    normal_hoop = inner(nh_c) + stiff_cross * strain_axial + stiff_hoop * strain_hoop
    strain_shear = (speed_axial[1:-1, 2:] - va_c) + (speed_hoop[2:, 1:-1] - vh_c)
    shear_stress = inner(ss_c) + stiff_shear * strain_shear
    return (va_c, vh_c, normal_axial, normal_hoop, shear_stress), m


def image_kernel(rows_ref, delays_ref, out_ref):
    pairs, pix_rows, pix_cols = delays_ref.shape
    lanes = rows_ref.shape[1]

    def body(k, acc):
        d = delays_ref[k]
        low = jnp.broadcast_to(rows_ref[pl.ds(2 * k, 1), :], (pix_rows, pix_cols))
        high = jnp.broadcast_to(rows_ref[pl.ds(2 * k + 1, 1), :], (pix_rows, pix_cols))
        idx = d & (lanes - 1)
        got_low = jnp.take_along_axis(low, idx, axis=1, mode="promise_in_bounds")
        got_high = jnp.take_along_axis(high, idx, axis=1, mode="promise_in_bounds")
        return acc + jnp.where(d >= lanes, got_high, got_low)

    acc = lax.fori_loop(0, pairs, body, jnp.zeros((pix_rows, pix_cols), jnp.float32), unroll=8)
    out_ref[...] = acc


def image(rows, delays):
    pairs, pix_rows, pix_cols = delays.shape
    return pl.pallas_call(
        image_kernel,
        out_shape=jax.ShapeDtypeStruct((pix_rows, pix_cols), jnp.float32),
        in_specs=[pl.BlockSpec(memory_space=pltpu.VMEM)] * 2,
        out_specs=pl.BlockSpec(memory_space=pltpu.VMEM),
        cost_estimate=pl.CostEstimate(
            flops=8 * pairs * pix_rows * pix_cols,
            bytes_accessed=4 * (rows.size + delays.size + pix_rows * pix_cols),
            transcendentals=0,
        ),
    )(rows, delays)


def gather_waves(local_waves):
    count = lax.axis_size("axial") * lax.axis_size("hoop")
    spread = jnp.broadcast_to(local_waves[None], (count,) + local_waves.shape)
    gathered = lax.all_to_all(spread, ("axial", "hoop"), 0, 0, tiled=True)
    return gathered.reshape((-1,) + local_waves.shape[1:])


def per_device(wave_state, layup_zone, moduli, sensors, history, receivers, delays):
    rows, cols = layup_zone.shape
    na = lax.axis_size("axial")
    stacked = jnp.concatenate(
        [wave_state[0], layup_zone.astype(jnp.float32)[None]], axis=0
    )
    padded = exchange(stacked, HALO)
    zone = padded[5].astype(jnp.int32)
    global_row = lax.axis_index("axial") * rows - HALO + lax.broadcasted_iota(
        jnp.int32, zone.shape, 0
    )
    inside = (global_row >= 0) & (global_row < na * rows)
    moduli_map = jnp.zeros((moduli.shape[1],) + zone.shape, jnp.float32)
    for zone_level in range(moduli.shape[0]):
        moduli_map = jnp.where(
            (zone == zone_level)[None], moduli[zone_level][:, None, None], moduli_map
        )
    moduli_map = jnp.where(inside[None], moduli_map, jnp.float32(0.0))
    fields = tuple(padded[c] for c in range(5))
    samples = []
    for step_index in range(STEPS):
        fields, moduli_map = advance(fields, moduli_map)
        moduli_map = [inner(m) for m in moduli_map]
        off = HALO - 2 * (step_index + 1)
        total = fields[2] + fields[3]
        tile = total[off:off + rows, off:off + cols]
        samples.append(tile.reshape(-1)[sensors])
        moduli_map = jnp.stack(moduli_map)
    next_state = jnp.stack(fields)[None]
    recorded = jnp.stack(samples, axis=1)[None]
    local_waves = jnp.concatenate([history[0], recorded[0]], axis=1)
    waveforms = gather_waves(local_waves)
    sample_count = waveforms.shape[1]
    chosen = waveforms[receivers[0]].reshape(2 * receivers.shape[1], sample_count // 2)
    partial_value = image(chosen, delays[0])
    summed = lax.psum(partial_value, "act")
    damage_map = summed * summed / (receivers.shape[1] * lax.axis_size("act"))
    return (next_state, recorded, damage_map)


def solution(mesh):
    return jax.shard_map(
        per_device,
        mesh=mesh,
        in_specs=(
            P("act", None, "axial", "hoop"),
            P("axial", "hoop"),
            P(),
            P(("axial", "hoop")),
            P("act", ("axial", "hoop"), None),
            P("act", None),
            P("act", None, "axial", "hoop"),
        ),
        out_specs=(
            P("act", None, "axial", "hoop"),
            P("act", ("axial", "hoop"), None),
            P("axial", "hoop"),
        ),
        check_vma=False,
    )
```

```python
import functools

import jax
import jax.numpy as jnp
from jax import lax
from jax.experimental import pallas as pl
from jax.experimental.pallas import tpu as pltpu
from jax.sharding import PartitionSpec as P

STEPS = 3
HALO = 2 * STEPS


def exchange(cells, halo):
    na = lax.axis_size("axial")
    nh = lax.axis_size("hoop")
    from_above = lax.ppermute(cells[:, -halo:, :], "axial", [(i, i + 1) for i in range(na - 1)])
    from_below = lax.ppermute(cells[:, :halo, :], "axial", [(i + 1, i) for i in range(na - 1)])
    cells = jnp.concatenate([from_above, cells, from_below], axis=1)
    from_left = lax.ppermute(cells[:, :, -halo:], "hoop", [(j, (j + 1) % nh) for j in range(nh)])
    from_right = lax.ppermute(cells[:, :, :halo], "hoop", [((j + 1) % nh, j) for j in range(nh)])
    return jnp.concatenate([from_left, cells, from_right], axis=2)


def inner(f):
    return f[1:-1, 1:-1]


def advance(fields, moduli_map):
    speed_axial, speed_hoop, normal_axial, normal_hoop, shear_stress = fields
    m = [inner(moduli_map[i]) for i in range(6)]
    mobility_axial, mobility_hoop = m[0], m[1]
    na_c = inner(normal_axial)
    nh_c = inner(normal_hoop)
    ss_c = inner(shear_stress)
    speed_axial = inner(speed_axial) + mobility_axial * (
        (normal_axial[2:, 1:-1] - na_c) + (ss_c - shear_stress[1:-1, :-2])
    )
    speed_hoop = inner(speed_hoop) + mobility_hoop * (
        (normal_hoop[1:-1, 2:] - nh_c) + (ss_c - shear_stress[:-2, 1:-1])
    )
    stiff_axial, stiff_cross, stiff_hoop, stiff_shear = (inner(m[i]) for i in range(2, 6))
    va_c = inner(speed_axial)
    vh_c = inner(speed_hoop)
    strain_axial = va_c - speed_axial[:-2, 1:-1]
    strain_hoop = vh_c - speed_hoop[1:-1, :-2]
    normal_axial = inner(na_c) + stiff_axial * strain_axial + stiff_cross * strain_hoop
    normal_hoop = inner(nh_c) + stiff_cross * strain_axial + stiff_hoop * strain_hoop
    strain_shear = (speed_axial[1:-1, 2:] - va_c) + (speed_hoop[2:, 1:-1] - vh_c)
    shear_stress = inner(ss_c) + stiff_shear * strain_shear
    return (va_c, vh_c, normal_axial, normal_hoop, shear_stress), m


def image_kernel(rows_ref, delays_ref, out_ref):
    pairs, pix_rows, pix_cols = delays_ref.shape
    lanes = rows_ref.shape[1]

    def body(k, acc):
        d = delays_ref[k]
        low = jnp.broadcast_to(rows_ref[pl.ds(2 * k, 1), :], (pix_rows, pix_cols))
        high = jnp.broadcast_to(rows_ref[pl.ds(2 * k + 1, 1), :], (pix_rows, pix_cols))
        idx = d & (lanes - 1)
        got_low = jnp.take_along_axis(low, idx, axis=1, mode="promise_in_bounds")
        got_high = jnp.take_along_axis(high, idx, axis=1, mode="promise_in_bounds")
        return acc + jnp.where(d >= lanes, got_high, got_low)

    acc = lax.fori_loop(0, pairs, body, jnp.zeros((pix_rows, pix_cols), jnp.float32), unroll=8)
    out_ref[...] = acc


def image(rows, delays):
    pairs, pix_rows, pix_cols = delays.shape
    return pl.pallas_call(
        image_kernel,
        out_shape=jax.ShapeDtypeStruct((pix_rows, pix_cols), jnp.float32),
        in_specs=[pl.BlockSpec(memory_space=pltpu.VMEM)] * 2,
        out_specs=pl.BlockSpec(memory_space=pltpu.VMEM),
        cost_estimate=pl.CostEstimate(
            flops=8 * pairs * pix_rows * pix_cols,
            bytes_accessed=4 * (rows.size + delays.size + pix_rows * pix_cols),
            transcendentals=0,
        ),
    )(rows, delays)


def a2a_gather(block, axes, count):
    spread = jnp.broadcast_to(block[None], (count,) + block.shape)
    gathered = lax.all_to_all(spread, axes, 0, 0, tiled=True)
    return gathered.reshape((-1,) + block.shape[1:])


def gather_waves(local_waves):
    inner_waves = a2a_gather(local_waves, "hoop", lax.axis_size("hoop"))
    return a2a_gather(inner_waves, "axial", lax.axis_size("axial"))


def per_device(wave_state, layup_zone, moduli, sensors, history, receivers, delays):
    rows, cols = layup_zone.shape
    na = lax.axis_size("axial")
    stacked = jnp.concatenate(
        [wave_state[0], layup_zone.astype(jnp.float32)[None]], axis=0
    )
    padded = exchange(stacked, HALO)
    zone = padded[5].astype(jnp.int32)
    global_row = lax.axis_index("axial") * rows - HALO + lax.broadcasted_iota(
        jnp.int32, zone.shape, 0
    )
    inside = (global_row >= 0) & (global_row < na * rows)
    moduli_map = jnp.zeros((moduli.shape[1],) + zone.shape, jnp.float32)
    for zone_level in range(moduli.shape[0]):
        moduli_map = jnp.where(
            (zone == zone_level)[None], moduli[zone_level][:, None, None], moduli_map
        )
    moduli_map = jnp.where(inside[None], moduli_map, jnp.float32(0.0))
    fields = tuple(padded[c] for c in range(5))
    samples = []
    for step_index in range(STEPS):
        fields, moduli_map = advance(fields, moduli_map)
        moduli_map = [inner(m) for m in moduli_map]
        off = HALO - 2 * (step_index + 1)
        total = fields[2] + fields[3]
        tile = total[off:off + rows, off:off + cols]
        samples.append(tile.reshape(-1)[sensors])
        moduli_map = jnp.stack(moduli_map)
    next_state = jnp.stack(fields)[None]
    recorded = jnp.stack(samples, axis=1)[None]
    local_waves = jnp.concatenate([history[0], recorded[0]], axis=1)
    waveforms = gather_waves(local_waves)
    sample_count = waveforms.shape[1]
    chosen = waveforms[receivers[0]].reshape(2 * receivers.shape[1], sample_count // 2)
    partial_value = image(chosen, delays[0])
    parts = lax.all_gather(partial_value, "act")
    summed = parts[0]
    for a in range(1, parts.shape[0]):
        summed = summed + parts[a]
    damage_map = summed * summed / (receivers.shape[1] * lax.axis_size("act"))
    return (next_state, recorded, damage_map)


def solution(mesh):
    return jax.shard_map(
        per_device,
        mesh=mesh,
        in_specs=(
            P("act", None, "axial", "hoop"),
            P("axial", "hoop"),
            P(),
            P(("axial", "hoop")),
            P("act", ("axial", "hoop"), None),
            P("act", None),
            P("act", None, "axial", "hoop"),
        ),
        out_specs=(
            P("act", None, "axial", "hoop"),
            P("act", ("axial", "hoop"), None),
            P("axial", "hoop"),
        ),
        check_vma=False,
    )
```

```python
import functools

import jax
import jax.numpy as jnp
from jax import lax
from jax.experimental import pallas as pl
from jax.experimental.pallas import tpu as pltpu
from jax.sharding import PartitionSpec as P

STEPS = 3
HALO = 2 * STEPS


def exchange(cells, zone, halo):
    na = lax.axis_size("axial")
    nh = lax.axis_size("hoop")

    def rows_of(lo, hi):
        return jnp.concatenate([cells[:, lo:hi, :], zone[None, lo:hi, :]], axis=0)

    rows = cells.shape[1]
    from_above = lax.ppermute(rows_of(rows - halo, rows), "axial", [(i, i + 1) for i in range(na - 1)])
    from_below = lax.ppermute(rows_of(0, halo), "axial", [(i + 1, i) for i in range(na - 1)])
    full = jnp.concatenate([from_above, rows_of(0, rows), from_below], axis=1)
    from_left = lax.ppermute(full[:, :, -halo:], "hoop", [(j, (j + 1) % nh) for j in range(nh)])
    from_right = lax.ppermute(full[:, :, :halo], "hoop", [((j + 1) % nh, j) for j in range(nh)])
    return jnp.concatenate([from_left, full, from_right], axis=2)


def inner(f):
    return f[1:-1, 1:-1]


def advance(fields, moduli_map):
    speed_axial, speed_hoop, normal_axial, normal_hoop, shear_stress = fields
    m = [inner(moduli_map[i]) for i in range(6)]
    mobility_axial, mobility_hoop = m[0], m[1]
    na_c = inner(normal_axial)
    nh_c = inner(normal_hoop)
    ss_c = inner(shear_stress)
    speed_axial = inner(speed_axial) + mobility_axial * (
        (normal_axial[2:, 1:-1] - na_c) + (ss_c - shear_stress[1:-1, :-2])
    )
    speed_hoop = inner(speed_hoop) + mobility_hoop * (
        (normal_hoop[1:-1, 2:] - nh_c) + (ss_c - shear_stress[:-2, 1:-1])
    )
    stiff_axial, stiff_cross, stiff_hoop, stiff_shear = (inner(m[i]) for i in range(2, 6))
    va_c = inner(speed_axial)
    vh_c = inner(speed_hoop)
    strain_axial = va_c - speed_axial[:-2, 1:-1]
    strain_hoop = vh_c - speed_hoop[1:-1, :-2]
    normal_axial = inner(na_c) + stiff_axial * strain_axial + stiff_cross * strain_hoop
    normal_hoop = inner(nh_c) + stiff_cross * strain_axial + stiff_hoop * strain_hoop
    strain_shear = (speed_axial[1:-1, 2:] - va_c) + (speed_hoop[2:, 1:-1] - vh_c)
    shear_stress = inner(ss_c) + stiff_shear * strain_shear
    return (va_c, vh_c, normal_axial, normal_hoop, shear_stress), m


def image_kernel(receivers_ref, waves_ref, delays_ref, out_ref):
    pairs, pix_rows, pix_cols = delays_ref.shape
    lanes = pix_cols
    tile = 8

    def body(k, acc):
        row = receivers_ref[k]
        base = pl.multiple_of((row // tile) * tile, tile)
        block = waves_ref[pl.ds(base, tile), :]
        pick = jnp.full(block.shape, row % tile, jnp.int32)
        spread = jnp.take_along_axis(block, pick, axis=0, mode="promise_in_bounds")
        low = spread[:, :lanes]
        high = spread[:, lanes:]
        parts = []
        for h in range(pix_rows // tile):
            d = delays_ref[k, pl.ds(h * tile, tile), :]
            idx = d & (lanes - 1)
            got_low = jnp.take_along_axis(low, idx, axis=1, mode="promise_in_bounds")
            got_high = jnp.take_along_axis(high, idx, axis=1, mode="promise_in_bounds")
            parts.append(jnp.where(d >= lanes, got_high, got_low))
        return acc + jnp.concatenate(parts, axis=0)

    acc = lax.fori_loop(0, pairs, body, jnp.zeros((pix_rows, pix_cols), jnp.float32), unroll=8)
    out_ref[...] = acc


def image(receivers, waves, delays):
    pairs, pix_rows, pix_cols = delays.shape
    return pl.pallas_call(
        image_kernel,
        out_shape=jax.ShapeDtypeStruct((pix_rows, pix_cols), jnp.float32),
        in_specs=[
            pl.BlockSpec(memory_space=pltpu.SMEM),
            pl.BlockSpec(memory_space=pltpu.VMEM),
            pl.BlockSpec(memory_space=pltpu.VMEM),
        ],
        out_specs=pl.BlockSpec(memory_space=pltpu.VMEM),
        cost_estimate=pl.CostEstimate(
            flops=8 * pairs * pix_rows * pix_cols,
            bytes_accessed=4 * (waves.size + delays.size + pix_rows * pix_cols),
            transcendentals=0,
        ),
    )(receivers, waves, delays)


def a2a_gather(block, axes, count):
    spread = jnp.broadcast_to(block[None], (count,) + block.shape)
    gathered = lax.all_to_all(spread, axes, 0, 0, tiled=True)
    return gathered.reshape((-1,) + block.shape[1:])


def gather_waves(local_waves):
    inner_waves = a2a_gather(local_waves, "hoop", lax.axis_size("hoop"))
    return a2a_gather(inner_waves, "axial", lax.axis_size("axial"))


def per_device(wave_state, layup_zone, moduli, sensors, history, receivers, delays):
    rows, cols = layup_zone.shape
    na = lax.axis_size("axial")
    padded = exchange(wave_state[0], layup_zone.astype(jnp.float32), HALO)
    zone = padded[5].astype(jnp.int32)
    global_row = lax.axis_index("axial") * rows - HALO + lax.broadcasted_iota(
        jnp.int32, zone.shape, 0
    )
    inside = (global_row >= 0) & (global_row < na * rows)
    moduli_map = jnp.zeros((moduli.shape[1],) + zone.shape, jnp.float32)
    for zone_level in range(moduli.shape[0]):
        moduli_map = jnp.where(
            (zone == zone_level)[None], moduli[zone_level][:, None, None], moduli_map
        )
    moduli_map = jnp.where(inside[None], moduli_map, jnp.float32(0.0))
    fields = tuple(padded[c] for c in range(5))
    totals = []
    for step_index in range(STEPS):
        fields, moduli_map = advance(fields, moduli_map)
        moduli_map = [inner(m) for m in moduli_map]
        off = HALO - 2 * (step_index + 1)
        total = fields[2] + fields[3]
        totals.append(total[off:off + rows, off:off + cols])
        moduli_map = jnp.stack(moduli_map)
    next_state = jnp.stack(fields)[None]
    recorded = jnp.stack(totals).reshape(STEPS, rows * cols)[:, sensors].T[None]
    local_waves = jnp.concatenate([history[0], recorded[0]], axis=1)
    waveforms = gather_waves(local_waves)
    partial_value = image(receivers[0], waveforms, delays[0])
    parts = lax.all_gather(partial_value, "act")
    summed = parts[0]
    for a in range(1, parts.shape[0]):
        summed = summed + parts[a]
    damage_map = summed * summed / (receivers.shape[1] * lax.axis_size("act"))
    return (next_state, recorded, damage_map)


def solution(mesh):
    return jax.shard_map(
        per_device,
        mesh=mesh,
        in_specs=(
            P("act", None, "axial", "hoop"),
            P("axial", "hoop"),
            P(),
            P(("axial", "hoop")),
            P("act", ("axial", "hoop"), None),
            P("act", None),
            P("act", None, "axial", "hoop"),
        ),
        out_specs=(
            P("act", None, "axial", "hoop"),
            P("act", ("axial", "hoop"), None),
            P("axial", "hoop"),
        ),
        check_vma=False,
    )
```

```python
import functools

import jax
import jax.numpy as jnp
from jax import lax
from jax.experimental import pallas as pl
from jax.experimental.pallas import tpu as pltpu
from jax.sharding import PartitionSpec as P

STEPS = 3
HALO = 2 * STEPS


def exchange(cells, halo):
    na = lax.axis_size("axial")
    nh = lax.axis_size("hoop")
    from_left = lax.ppermute(cells[:, :, -halo:], "hoop", [(j, (j + 1) % nh) for j in range(nh)])
    from_right = lax.ppermute(cells[:, :, :halo], "hoop", [((j + 1) % nh, j) for j in range(nh)])
    cells = jnp.concatenate([from_left, cells, from_right], axis=2)
    from_above = lax.ppermute(cells[:, -halo:, :], "axial", [(i, i + 1) for i in range(na - 1)])
    from_below = lax.ppermute(cells[:, :halo, :], "axial", [(i + 1, i) for i in range(na - 1)])
    return jnp.concatenate([from_above, cells, from_below], axis=1)


def inner(f):
    return f[1:-1, 1:-1]


def advance(fields, moduli_map):
    speed_axial, speed_hoop, normal_axial, normal_hoop, shear_stress = fields
    m = [inner(moduli_map[i]) for i in range(6)]
    mobility_axial, mobility_hoop = m[0], m[1]
    na_c = inner(normal_axial)
    nh_c = inner(normal_hoop)
    ss_c = inner(shear_stress)
    speed_axial = inner(speed_axial) + mobility_axial * (
        (normal_axial[2:, 1:-1] - na_c) + (ss_c - shear_stress[1:-1, :-2])
    )
    speed_hoop = inner(speed_hoop) + mobility_hoop * (
        (normal_hoop[1:-1, 2:] - nh_c) + (ss_c - shear_stress[:-2, 1:-1])
    )
    stiff_axial, stiff_cross, stiff_hoop, stiff_shear = (inner(m[i]) for i in range(2, 6))
    va_c = inner(speed_axial)
    vh_c = inner(speed_hoop)
    strain_axial = va_c - speed_axial[:-2, 1:-1]
    strain_hoop = vh_c - speed_hoop[1:-1, :-2]
    normal_axial = inner(na_c) + stiff_axial * strain_axial + stiff_cross * strain_hoop
    normal_hoop = inner(nh_c) + stiff_cross * strain_axial + stiff_hoop * strain_hoop
    strain_shear = (speed_axial[1:-1, 2:] - va_c) + (speed_hoop[2:, 1:-1] - vh_c)
    shear_stress = inner(ss_c) + stiff_shear * strain_shear
    return (va_c, vh_c, normal_axial, normal_hoop, shear_stress), m


def image_kernel(receivers_ref, waves_ref, delays_ref, out_ref):
    pairs, pix_rows, pix_cols = delays_ref.shape
    lanes = pix_cols
    tile = 8

    def body(k, acc):
        row = receivers_ref[k]
        base = pl.multiple_of((row // tile) * tile, tile)
        block = waves_ref[pl.ds(base, tile), :]
        pick = jnp.full(block.shape, row % tile, jnp.int32)
        spread = jnp.take_along_axis(block, pick, axis=0, mode="promise_in_bounds")
        low = spread[:, :lanes]
        high = spread[:, lanes:]
        parts = []
        for h in range(pix_rows // tile):
            d = delays_ref[k, pl.ds(h * tile, tile), :]
            idx = d & (lanes - 1)
            got_low = jnp.take_along_axis(low, idx, axis=1, mode="promise_in_bounds")
            got_high = jnp.take_along_axis(high, idx, axis=1, mode="promise_in_bounds")
            parts.append(jnp.where(d >= lanes, got_high, got_low))
        return acc + jnp.concatenate(parts, axis=0)

    acc = lax.fori_loop(0, pairs, body, jnp.zeros((pix_rows, pix_cols), jnp.float32), unroll=8)
    out_ref[...] = acc


def image(receivers, waves, delays):
    pairs, pix_rows, pix_cols = delays.shape
    return pl.pallas_call(
        image_kernel,
        out_shape=jax.ShapeDtypeStruct((pix_rows, pix_cols), jnp.float32),
        in_specs=[
            pl.BlockSpec(memory_space=pltpu.SMEM),
            pl.BlockSpec(memory_space=pltpu.VMEM),
            pl.BlockSpec(memory_space=pltpu.VMEM),
        ],
        out_specs=pl.BlockSpec(memory_space=pltpu.VMEM),
        cost_estimate=pl.CostEstimate(
            flops=8 * pairs * pix_rows * pix_cols,
            bytes_accessed=4 * (waves.size + delays.size + pix_rows * pix_cols),
            transcendentals=0,
        ),
    )(receivers, waves, delays)


def a2a_gather(block, axes, count):
    spread = jnp.broadcast_to(block[None], (count,) + block.shape)
    gathered = lax.all_to_all(spread, axes, 0, 0, tiled=True)
    return gathered.reshape((-1,) + block.shape[1:])


def gather_waves(local_waves):
    inner_waves = a2a_gather(local_waves, "hoop", lax.axis_size("hoop"))
    return a2a_gather(inner_waves, "axial", lax.axis_size("axial"))


def per_device(wave_state, layup_zone, moduli, sensors, history, receivers, delays):
    rows, cols = layup_zone.shape
    na = lax.axis_size("axial")
    stacked = jnp.concatenate(
        [wave_state[0], layup_zone.astype(jnp.float32)[None]], axis=0
    )
    padded = exchange(stacked, HALO)
    zone = padded[5].astype(jnp.int32)
    global_row = lax.axis_index("axial") * rows - HALO + lax.broadcasted_iota(
        jnp.int32, zone.shape, 0
    )
    inside = (global_row >= 0) & (global_row < na * rows)
    moduli_map = jnp.zeros((moduli.shape[1],) + zone.shape, jnp.float32)
    for zone_level in range(moduli.shape[0]):
        moduli_map = jnp.where(
            (zone == zone_level)[None], moduli[zone_level][:, None, None], moduli_map
        )
    moduli_map = jnp.where(inside[None], moduli_map, jnp.float32(0.0))
    fields = tuple(padded[c] for c in range(5))
    samples = []
    for step_index in range(STEPS):
        fields, moduli_map = advance(fields, moduli_map)
        moduli_map = [inner(m) for m in moduli_map]
        off = HALO - 2 * (step_index + 1)
        total = fields[2] + fields[3]
        tile = total[off:off + rows, off:off + cols]
        samples.append(tile.reshape(-1)[sensors])
        moduli_map = jnp.stack(moduli_map)
    next_state = jnp.stack(fields)[None]
    recorded = jnp.stack(samples, axis=1)[None]
    local_waves = jnp.concatenate([history[0], recorded[0]], axis=1)
    waveforms = gather_waves(local_waves)
    partial_value = image(receivers[0], waveforms, delays[0])
    parts = lax.all_gather(partial_value, "act")
    summed = parts[0]
    for a in range(1, parts.shape[0]):
        summed = summed + parts[a]
    damage_map = summed * summed / (receivers.shape[1] * lax.axis_size("act"))
    return (next_state, recorded, damage_map)


def solution(mesh):
    return jax.shard_map(
        per_device,
        mesh=mesh,
        in_specs=(
            P("act", None, "axial", "hoop"),
            P("axial", "hoop"),
            P(),
            P(("axial", "hoop")),
            P("act", ("axial", "hoop"), None),
            P("act", None),
            P("act", None, "axial", "hoop"),
        ),
        out_specs=(
            P("act", None, "axial", "hoop"),
            P("act", ("axial", "hoop"), None),
            P("axial", "hoop"),
        ),
        check_vma=False,
    )
```

```python
import functools

import jax
import jax.numpy as jnp
from jax import lax
from jax.experimental import pallas as pl
from jax.experimental.pallas import tpu as pltpu
from jax.sharding import PartitionSpec as P

STEPS = 3
HALO = 2 * STEPS


def exchange(cells, halo):
    na = lax.axis_size("axial")
    nh = lax.axis_size("hoop")
    from_left = lax.ppermute(cells[:, :, -halo:], "hoop", [(j, (j + 1) % nh) for j in range(nh)])
    from_right = lax.ppermute(cells[:, :, :halo], "hoop", [((j + 1) % nh, j) for j in range(nh)])
    cells = jnp.concatenate([from_left, cells, from_right], axis=2)
    from_above = lax.ppermute(cells[:, -halo:, :], "axial", [(i, i + 1) for i in range(na - 1)])
    from_below = lax.ppermute(cells[:, :halo, :], "axial", [(i + 1, i) for i in range(na - 1)])
    return jnp.concatenate([from_above, cells, from_below], axis=1)


def inner(f):
    return f[1:-1, 1:-1]


def advance(fields, moduli_map):
    speed_axial, speed_hoop, normal_axial, normal_hoop, shear_stress = fields
    m = [inner(moduli_map[i]) for i in range(6)]
    mobility_axial, mobility_hoop = m[0], m[1]
    na_c = inner(normal_axial)
    nh_c = inner(normal_hoop)
    ss_c = inner(shear_stress)
    speed_axial = inner(speed_axial) + mobility_axial * (
        (normal_axial[2:, 1:-1] - na_c) + (ss_c - shear_stress[1:-1, :-2])
    )
    speed_hoop = inner(speed_hoop) + mobility_hoop * (
        (normal_hoop[1:-1, 2:] - nh_c) + (ss_c - shear_stress[:-2, 1:-1])
    )
    stiff_axial, stiff_cross, stiff_hoop, stiff_shear = (inner(m[i]) for i in range(2, 6))
    va_c = inner(speed_axial)
    vh_c = inner(speed_hoop)
    strain_axial = va_c - speed_axial[:-2, 1:-1]
    strain_hoop = vh_c - speed_hoop[1:-1, :-2]
    normal_axial = inner(na_c) + stiff_axial * strain_axial + stiff_cross * strain_hoop
    normal_hoop = inner(nh_c) + stiff_cross * strain_axial + stiff_hoop * strain_hoop
    strain_shear = (speed_axial[1:-1, 2:] - va_c) + (speed_hoop[2:, 1:-1] - vh_c)
    shear_stress = inner(ss_c) + stiff_shear * strain_shear
    return (va_c, vh_c, normal_axial, normal_hoop, shear_stress), m


def image_kernel(receivers_ref, waves_ref, delays_ref, out_ref):
    pairs, pix_rows, pix_cols = delays_ref.shape
    lanes = pix_cols
    tile = 8

    def body(k, acc):
        row = receivers_ref[k]
        base = pl.multiple_of((row // tile) * tile, tile)
        block = waves_ref[pl.ds(base, tile), :]
        pick = jnp.full(block.shape, row % tile, jnp.int32)
        spread = jnp.take_along_axis(block, pick, axis=0, mode="promise_in_bounds")
        low = spread[:, :lanes]
        high = spread[:, lanes:]
        parts = []
        for h in range(pix_rows // tile):
            d = delays_ref[k, pl.ds(h * tile, tile), :]
            idx = d & (lanes - 1)
            got_low = jnp.take_along_axis(low, idx, axis=1, mode="promise_in_bounds")
            got_high = jnp.take_along_axis(high, idx, axis=1, mode="promise_in_bounds")
            parts.append(jnp.where(d >= lanes, got_high, got_low))
        return acc + jnp.concatenate(parts, axis=0)

    acc = lax.fori_loop(0, pairs, body, jnp.zeros((pix_rows, pix_cols), jnp.float32), unroll=16)
    out_ref[...] = acc


def image(receivers, waves, delays):
    pairs, pix_rows, pix_cols = delays.shape
    return pl.pallas_call(
        image_kernel,
        out_shape=jax.ShapeDtypeStruct((pix_rows, pix_cols), jnp.float32),
        in_specs=[
            pl.BlockSpec(memory_space=pltpu.SMEM),
            pl.BlockSpec(memory_space=pltpu.VMEM),
            pl.BlockSpec(memory_space=pltpu.VMEM),
        ],
        out_specs=pl.BlockSpec(memory_space=pltpu.VMEM),
        cost_estimate=pl.CostEstimate(
            flops=8 * pairs * pix_rows * pix_cols,
            bytes_accessed=4 * (waves.size + delays.size + pix_rows * pix_cols),
            transcendentals=0,
        ),
    )(receivers, waves, delays)


def a2a_gather(block, axes, count):
    spread = jnp.broadcast_to(block[None], (count,) + block.shape)
    gathered = lax.all_to_all(spread, axes, 0, 0, tiled=True)
    return gathered.reshape((-1,) + block.shape[1:])


def gather_waves(local_waves):
    inner_waves = a2a_gather(local_waves, "hoop", lax.axis_size("hoop"))
    return a2a_gather(inner_waves, "axial", lax.axis_size("axial"))


def per_device(wave_state, layup_zone, moduli, sensors, history, receivers, delays):
    rows, cols = layup_zone.shape
    na = lax.axis_size("axial")
    stacked = jnp.concatenate(
        [wave_state[0], layup_zone.astype(jnp.float32)[None]], axis=0
    )
    padded = exchange(stacked, HALO)
    zone = padded[5].astype(jnp.int32)
    global_row = lax.axis_index("axial") * rows - HALO + lax.broadcasted_iota(
        jnp.int32, zone.shape, 0
    )
    inside = (global_row >= 0) & (global_row < na * rows)
    moduli_map = jnp.zeros((moduli.shape[1],) + zone.shape, jnp.float32)
    for zone_level in range(moduli.shape[0]):
        moduli_map = jnp.where(
            (zone == zone_level)[None], moduli[zone_level][:, None, None], moduli_map
        )
    moduli_map = jnp.where(inside[None], moduli_map, jnp.float32(0.0))
    fields = tuple(padded[c] for c in range(5))
    samples = []
    for step_index in range(STEPS):
        fields, moduli_map = advance(fields, moduli_map)
        moduli_map = [inner(m) for m in moduli_map]
        off = HALO - 2 * (step_index + 1)
        total = fields[2] + fields[3]
        tile = total[off:off + rows, off:off + cols]
        samples.append(tile.reshape(-1)[sensors])
        moduli_map = jnp.stack(moduli_map)
    next_state = jnp.stack(fields)[None]
    recorded = jnp.stack(samples, axis=1)[None]
    local_waves = jnp.concatenate([history[0], recorded[0]], axis=1)
    waveforms = gather_waves(local_waves)
    partial_value = image(receivers[0], waveforms, delays[0])
    parts = lax.all_gather(partial_value.reshape(-1), "act").reshape((-1,) + partial_value.shape)
    summed = parts[0]
    for a in range(1, parts.shape[0]):
        summed = summed + parts[a]
    damage_map = summed * summed / (receivers.shape[1] * lax.axis_size("act"))
    return (next_state, recorded, damage_map)


def solution(mesh):
    return jax.shard_map(
        per_device,
        mesh=mesh,
        in_specs=(
            P("act", None, "axial", "hoop"),
            P("axial", "hoop"),
            P(),
            P(("axial", "hoop")),
            P("act", ("axial", "hoop"), None),
            P("act", None),
            P("act", None, "axial", "hoop"),
        ),
        out_specs=(
            P("act", None, "axial", "hoop"),
            P("act", ("axial", "hoop"), None),
            P("axial", "hoop"),
        ),
        check_vma=False,
    )
```

```python
import functools

import jax
import jax.numpy as jnp
from jax import lax
from jax.experimental import pallas as pl
from jax.experimental.pallas import tpu as pltpu
from jax.sharding import PartitionSpec as P

STEPS = 3
HALO = 2 * STEPS


def exchange(cells, halo):
    na = lax.axis_size("axial")
    nh = lax.axis_size("hoop")
    from_left = lax.ppermute(cells[:, :, -halo:], "hoop", [(j, (j + 1) % nh) for j in range(nh)])
    from_right = lax.ppermute(cells[:, :, :halo], "hoop", [((j + 1) % nh, j) for j in range(nh)])
    cells = jnp.concatenate([from_left, cells, from_right], axis=2)
    from_above = lax.ppermute(cells[:, -halo:, :], "axial", [(i, i + 1) for i in range(na - 1)])
    from_below = lax.ppermute(cells[:, :halo, :], "axial", [(i + 1, i) for i in range(na - 1)])
    return jnp.concatenate([from_above, cells, from_below], axis=1)


def inner(f):
    return f[1:-1, 1:-1]


def advance(fields, moduli_map):
    speed_axial, speed_hoop, normal_axial, normal_hoop, shear_stress = fields
    m = [inner(moduli_map[i]) for i in range(6)]
    mobility_axial, mobility_hoop = m[0], m[1]
    na_c = inner(normal_axial)
    nh_c = inner(normal_hoop)
    ss_c = inner(shear_stress)
    speed_axial = inner(speed_axial) + mobility_axial * (
        (normal_axial[2:, 1:-1] - na_c) + (ss_c - shear_stress[1:-1, :-2])
    )
    speed_hoop = inner(speed_hoop) + mobility_hoop * (
        (normal_hoop[1:-1, 2:] - nh_c) + (ss_c - shear_stress[:-2, 1:-1])
    )
    stiff_axial, stiff_cross, stiff_hoop, stiff_shear = (inner(m[i]) for i in range(2, 6))
    va_c = inner(speed_axial)
    vh_c = inner(speed_hoop)
    strain_axial = va_c - speed_axial[:-2, 1:-1]
    strain_hoop = vh_c - speed_hoop[1:-1, :-2]
    normal_axial = inner(na_c) + stiff_axial * strain_axial + stiff_cross * strain_hoop
    normal_hoop = inner(nh_c) + stiff_cross * strain_axial + stiff_hoop * strain_hoop
    strain_shear = (speed_axial[1:-1, 2:] - va_c) + (speed_hoop[2:, 1:-1] - vh_c)
    shear_stress = inner(ss_c) + stiff_shear * strain_shear
    return (va_c, vh_c, normal_axial, normal_hoop, shear_stress), m


def image_kernel(receivers_ref, waves_ref, delays_ref, out_ref):
    pairs, pix_rows, pix_cols = delays_ref.shape
    lanes = pix_cols
    tile = 8

    def body(k, acc):
        row = receivers_ref[k]
        base = pl.multiple_of((row // tile) * tile, tile)
        block = waves_ref[pl.ds(base, tile), :]
        pick = jnp.full(block.shape, row % tile, jnp.int32)
        spread = jnp.take_along_axis(block, pick, axis=0, mode="promise_in_bounds")
        low = spread[:, :lanes]
        high = spread[:, lanes:]
        parts = []
        for h in range(pix_rows // tile):
            d = delays_ref[k, pl.ds(h * tile, tile), :]
            idx = d & (lanes - 1)
            got_low = jnp.take_along_axis(low, idx, axis=1, mode="promise_in_bounds")
            got_high = jnp.take_along_axis(high, idx, axis=1, mode="promise_in_bounds")
            parts.append(jnp.where(d >= lanes, got_high, got_low))
        return acc + jnp.concatenate(parts, axis=0)

    acc = lax.fori_loop(0, pairs, body, jnp.zeros((pix_rows, pix_cols), jnp.float32), unroll=16)
    out_ref[...] = acc


def image(receivers, waves, delays):
    pairs, pix_rows, pix_cols = delays.shape
    return pl.pallas_call(
        image_kernel,
        out_shape=jax.ShapeDtypeStruct((pix_rows, pix_cols), jnp.float32),
        in_specs=[
            pl.BlockSpec(memory_space=pltpu.SMEM),
            pl.BlockSpec(memory_space=pltpu.VMEM),
            pl.BlockSpec(memory_space=pltpu.VMEM),
        ],
        out_specs=pl.BlockSpec(memory_space=pltpu.VMEM),
        cost_estimate=pl.CostEstimate(
            flops=8 * pairs * pix_rows * pix_cols,
            bytes_accessed=4 * (waves.size + delays.size + pix_rows * pix_cols),
            transcendentals=0,
        ),
    )(receivers, waves, delays)


def a2a_gather(block, axes, count):
    spread = jnp.broadcast_to(block[None], (count,) + block.shape)
    gathered = lax.all_to_all(spread, axes, 0, 0, tiled=True)
    return gathered.reshape((-1,) + block.shape[1:])


def gather_waves(local_waves):
    inner_waves = a2a_gather(local_waves, "hoop", lax.axis_size("hoop"))
    return a2a_gather(inner_waves, "axial", lax.axis_size("axial"))


def per_device(wave_state, layup_zone, moduli, sensors, history, receivers, delays):
    rows, cols = layup_zone.shape
    na = lax.axis_size("axial")
    stacked = jnp.concatenate(
        [wave_state[0], layup_zone.astype(jnp.float32)[None]], axis=0
    )
    padded = exchange(stacked, HALO)
    zone = padded[5].astype(jnp.int32)
    global_row = lax.axis_index("axial") * rows - HALO + lax.broadcasted_iota(
        jnp.int32, zone.shape, 0
    )
    inside = (global_row >= 0) & (global_row < na * rows)
    moduli_map = jnp.zeros((moduli.shape[1],) + zone.shape, jnp.float32)
    for zone_level in range(moduli.shape[0]):
        moduli_map = jnp.where(
            (zone == zone_level)[None], moduli[zone_level][:, None, None], moduli_map
        )
    moduli_map = jnp.where(inside[None], moduli_map, jnp.float32(0.0))
    fields = tuple(padded[c] for c in range(5))
    samples = []
    for step_index in range(STEPS):
        fields, moduli_map = advance(fields, moduli_map)
        moduli_map = [inner(m) for m in moduli_map]
        off = HALO - 2 * (step_index + 1)
        total = fields[2] + fields[3]
        tile = total[off:off + rows, off:off + cols]
        flat = tile.reshape(1, -1)
        cell = lax.broadcasted_iota(jnp.int32, (sensors.shape[0], flat.shape[1]), 1)
        hit = cell == sensors[:, None]
        samples.append(jnp.sum(jnp.where(hit, flat, jnp.float32(0.0)), axis=1))
        moduli_map = jnp.stack(moduli_map)
    next_state = jnp.stack(fields)[None]
    recorded = jnp.stack(samples, axis=1)[None]
    local_waves = jnp.concatenate([history[0], recorded[0]], axis=1)
    waveforms = gather_waves(local_waves)
    partial_value = image(receivers[0], waveforms, delays[0])
    parts = lax.all_gather(partial_value.reshape(-1), "act").reshape((-1,) + partial_value.shape)
    summed = parts[0]
    for a in range(1, parts.shape[0]):
        summed = summed + parts[a]
    damage_map = summed * summed / (receivers.shape[1] * lax.axis_size("act"))
    return (next_state, recorded, damage_map)


def solution(mesh):
    return jax.shard_map(
        per_device,
        mesh=mesh,
        in_specs=(
            P("act", None, "axial", "hoop"),
            P("axial", "hoop"),
            P(),
            P(("axial", "hoop")),
            P("act", ("axial", "hoop"), None),
            P("act", None),
            P("act", None, "axial", "hoop"),
        ),
        out_specs=(
            P("act", None, "axial", "hoop"),
            P("act", ("axial", "hoop"), None),
            P("axial", "hoop"),
        ),
        check_vma=False,
    )
```

```python
import functools

import jax
import jax.numpy as jnp
from jax import lax
from jax.experimental import pallas as pl
from jax.experimental.pallas import tpu as pltpu
from jax.sharding import PartitionSpec as P

STEPS = 3
HALO = 2 * STEPS


def exchange(cells, halo):
    na = lax.axis_size("axial")
    nh = lax.axis_size("hoop")
    from_left = lax.ppermute(cells[:, :, -halo:], "hoop", [(j, (j + 1) % nh) for j in range(nh)])
    from_right = lax.ppermute(cells[:, :, :halo], "hoop", [((j + 1) % nh, j) for j in range(nh)])
    cells = jnp.concatenate([from_left, cells, from_right], axis=2)
    from_above = lax.ppermute(cells[:, -halo:, :], "axial", [(i, i + 1) for i in range(na - 1)])
    from_below = lax.ppermute(cells[:, :halo, :], "axial", [(i + 1, i) for i in range(na - 1)])
    return jnp.concatenate([from_above, cells, from_below], axis=1)


def inner(f):
    return f[1:-1, 1:-1]


def advance(fields, moduli_map):
    speed_axial, speed_hoop, normal_axial, normal_hoop, shear_stress = fields
    m = [inner(moduli_map[i]) for i in range(6)]
    mobility_axial, mobility_hoop = m[0], m[1]
    na_c = inner(normal_axial)
    nh_c = inner(normal_hoop)
    ss_c = inner(shear_stress)
    speed_axial = inner(speed_axial) + mobility_axial * (
        (normal_axial[2:, 1:-1] - na_c) + (ss_c - shear_stress[1:-1, :-2])
    )
    speed_hoop = inner(speed_hoop) + mobility_hoop * (
        (normal_hoop[1:-1, 2:] - nh_c) + (ss_c - shear_stress[:-2, 1:-1])
    )
    stiff_axial, stiff_cross, stiff_hoop, stiff_shear = (inner(m[i]) for i in range(2, 6))
    va_c = inner(speed_axial)
    vh_c = inner(speed_hoop)
    strain_axial = va_c - speed_axial[:-2, 1:-1]
    strain_hoop = vh_c - speed_hoop[1:-1, :-2]
    normal_axial = inner(na_c) + stiff_axial * strain_axial + stiff_cross * strain_hoop
    normal_hoop = inner(nh_c) + stiff_cross * strain_axial + stiff_hoop * strain_hoop
    strain_shear = (speed_axial[1:-1, 2:] - va_c) + (speed_hoop[2:, 1:-1] - vh_c)
    shear_stress = inner(ss_c) + stiff_shear * strain_shear
    return (va_c, vh_c, normal_axial, normal_hoop, shear_stress), m


def image_kernel(receivers_ref, waves_ref, delays_ref, out_ref):
    pairs, pix_rows, pix_cols = delays_ref.shape
    lanes = pix_cols
    tile = 8

    def body(k, acc):
        row = receivers_ref[k]
        base = pl.multiple_of((row // tile) * tile, tile)
        block = waves_ref[pl.ds(base, tile), :]
        pick = jnp.full(block.shape, row % tile, jnp.int32)
        spread = jnp.take_along_axis(block, pick, axis=0, mode="promise_in_bounds")
        low = spread[:, :lanes]
        high = spread[:, lanes:]
        parts = []
        for h in range(pix_rows // tile):
            d = delays_ref[k, pl.ds(h * tile, tile), :]
            idx = d & (lanes - 1)
            got_low = jnp.take_along_axis(low, idx, axis=1, mode="promise_in_bounds")
            got_high = jnp.take_along_axis(high, idx, axis=1, mode="promise_in_bounds")
            parts.append(jnp.where(d >= lanes, got_high, got_low))
        return acc + jnp.concatenate(parts, axis=0)

    acc = lax.fori_loop(0, pairs, body, jnp.zeros((pix_rows, pix_cols), jnp.float32), unroll=16)
    out_ref[...] = acc


def image(receivers, waves, delays):
    pairs, pix_rows, pix_cols = delays.shape
    return pl.pallas_call(
        image_kernel,
        out_shape=jax.ShapeDtypeStruct((pix_rows, pix_cols), jnp.float32),
        in_specs=[
            pl.BlockSpec(memory_space=pltpu.SMEM),
            pl.BlockSpec(memory_space=pltpu.VMEM),
            pl.BlockSpec(memory_space=pltpu.VMEM),
        ],
        out_specs=pl.BlockSpec(memory_space=pltpu.VMEM),
        cost_estimate=pl.CostEstimate(
            flops=8 * pairs * pix_rows * pix_cols,
            bytes_accessed=4 * (waves.size + delays.size + pix_rows * pix_cols),
            transcendentals=0,
        ),
    )(receivers, waves, delays)


def a2a_gather(block, axes, count):
    spread = jnp.broadcast_to(block[None], (count,) + block.shape)
    gathered = lax.all_to_all(spread, axes, 0, 0, tiled=True)
    return gathered.reshape((-1,) + block.shape[1:])


def gather_waves(local_waves):
    inner_waves = a2a_gather(local_waves, "hoop", lax.axis_size("hoop"))
    return a2a_gather(inner_waves, "axial", lax.axis_size("axial"))


def per_device(wave_state, layup_zone, moduli, sensors, history, receivers, delays):
    rows, cols = layup_zone.shape
    na = lax.axis_size("axial")
    stacked = jnp.concatenate(
        [wave_state[0], layup_zone.astype(jnp.float32)[None]], axis=0
    )
    hist = history[0]
    hist_count = hist.shape[1]
    hist_wide = jnp.concatenate(
        [hist, jnp.zeros((hist.shape[0], STEPS), jnp.float32)], axis=1
    )
    cell = lax.broadcasted_iota(jnp.int32, (sensors.shape[0], rows * cols), 1)
    hit = cell == sensors[:, None]
    stacked, hist_wide, hit = lax.optimization_barrier((stacked, hist_wide, hit))
    padded = exchange(stacked, HALO)
    zone = padded[5].astype(jnp.int32)
    global_row = lax.axis_index("axial") * rows - HALO + lax.broadcasted_iota(
        jnp.int32, zone.shape, 0
    )
    inside = (global_row >= 0) & (global_row < na * rows)
    moduli_map = jnp.zeros((moduli.shape[1],) + zone.shape, jnp.float32)
    for zone_level in range(moduli.shape[0]):
        moduli_map = jnp.where(
            (zone == zone_level)[None], moduli[zone_level][:, None, None], moduli_map
        )
    moduli_map = jnp.where(inside[None], moduli_map, jnp.float32(0.0))
    fields = tuple(padded[c] for c in range(5))
    samples = []
    for step_index in range(STEPS):
        fields, moduli_map = advance(fields, moduli_map)
        moduli_map = [inner(m) for m in moduli_map]
        off = HALO - 2 * (step_index + 1)
        total = fields[2] + fields[3]
        tile = total[off:off + rows, off:off + cols]
        flat = tile.reshape(1, -1)
        samples.append(jnp.sum(jnp.where(hit, flat, jnp.float32(0.0)), axis=1))
        moduli_map = jnp.stack(moduli_map)
    next_state = jnp.stack(fields)[None]
    recorded = jnp.stack(samples, axis=1)[None]
    column = lax.broadcasted_iota(jnp.int32, hist_wide.shape, 1)
    trace_wide = jnp.pad(recorded[0], ((0, 0), (hist_count, 0)))
    local_waves = jnp.where(column >= hist_count, trace_wide, hist_wide)
    waveforms = gather_waves(local_waves)
    partial_value = image(receivers[0], waveforms, delays[0])
    parts = lax.all_gather(partial_value.reshape(-1), "act").reshape((-1,) + partial_value.shape)
    summed = parts[0]
    for a in range(1, parts.shape[0]):
        summed = summed + parts[a]
    damage_map = summed * summed / (receivers.shape[1] * lax.axis_size("act"))
    return (next_state, recorded, damage_map)


def solution(mesh):
    return jax.shard_map(
        per_device,
        mesh=mesh,
        in_specs=(
            P("act", None, "axial", "hoop"),
            P("axial", "hoop"),
            P(),
            P(("axial", "hoop")),
            P("act", ("axial", "hoop"), None),
            P("act", None),
            P("act", None, "axial", "hoop"),
        ),
        out_specs=(
            P("act", None, "axial", "hoop"),
            P("act", ("axial", "hoop"), None),
            P("axial", "hoop"),
        ),
        check_vma=False,
    )
```

```python
import functools

import jax
import jax.numpy as jnp
from jax import lax
from jax.experimental import pallas as pl
from jax.experimental.pallas import tpu as pltpu
from jax.sharding import PartitionSpec as P

STEPS = 3
HALO = 2 * STEPS


def exchange(cells, halo):
    na = lax.axis_size("axial")
    nh = lax.axis_size("hoop")
    from_left = lax.ppermute(cells[:, :, -halo:], "hoop", [(j, (j + 1) % nh) for j in range(nh)])
    from_right = lax.ppermute(cells[:, :, :halo], "hoop", [((j + 1) % nh, j) for j in range(nh)])
    cells = jnp.concatenate([from_left, cells, from_right], axis=2)
    from_above = lax.ppermute(cells[:, -halo:, :], "axial", [(i, i + 1) for i in range(na - 1)])
    from_below = lax.ppermute(cells[:, :halo, :], "axial", [(i + 1, i) for i in range(na - 1)])
    return jnp.concatenate([from_above, cells, from_below], axis=1)


def inner(f):
    return f[1:-1, 1:-1]


def advance(fields, moduli_map):
    speed_axial, speed_hoop, normal_axial, normal_hoop, shear_stress = fields
    m = [inner(moduli_map[i]) for i in range(6)]
    mobility_axial, mobility_hoop = m[0], m[1]
    na_c = inner(normal_axial)
    nh_c = inner(normal_hoop)
    ss_c = inner(shear_stress)
    speed_axial = inner(speed_axial) + mobility_axial * (
        (normal_axial[2:, 1:-1] - na_c) + (ss_c - shear_stress[1:-1, :-2])
    )
    speed_hoop = inner(speed_hoop) + mobility_hoop * (
        (normal_hoop[1:-1, 2:] - nh_c) + (ss_c - shear_stress[:-2, 1:-1])
    )
    stiff_axial, stiff_cross, stiff_hoop, stiff_shear = (inner(m[i]) for i in range(2, 6))
    va_c = inner(speed_axial)
    vh_c = inner(speed_hoop)
    strain_axial = va_c - speed_axial[:-2, 1:-1]
    strain_hoop = vh_c - speed_hoop[1:-1, :-2]
    normal_axial = inner(na_c) + stiff_axial * strain_axial + stiff_cross * strain_hoop
    normal_hoop = inner(nh_c) + stiff_cross * strain_axial + stiff_hoop * strain_hoop
    strain_shear = (speed_axial[1:-1, 2:] - va_c) + (speed_hoop[2:, 1:-1] - vh_c)
    shear_stress = inner(ss_c) + stiff_shear * strain_shear
    return (va_c, vh_c, normal_axial, normal_hoop, shear_stress), m


def image_kernel(receivers_ref, waves_ref, delays_ref, out_ref):
    pairs, pix_rows, pix_cols = delays_ref.shape
    lanes = pix_cols
    tile = 8

    def body(k, acc):
        row = receivers_ref[k]
        base = pl.multiple_of((row // tile) * tile, tile)
        block = waves_ref[pl.ds(base, tile), :]
        pick = jnp.full(block.shape, row % tile, jnp.int32)
        spread = jnp.take_along_axis(block, pick, axis=0, mode="promise_in_bounds")
        low = spread[:, :lanes]
        high = spread[:, lanes:]
        parts = []
        for h in range(pix_rows // tile):
            d = delays_ref[k, pl.ds(h * tile, tile), :]
            idx = d & (lanes - 1)
            got_low = jnp.take_along_axis(low, idx, axis=1, mode="promise_in_bounds")
            got_high = jnp.take_along_axis(high, idx, axis=1, mode="promise_in_bounds")
            parts.append(jnp.where(d >= lanes, got_high, got_low))
        return acc + jnp.concatenate(parts, axis=0)

    acc = lax.fori_loop(0, pairs, body, jnp.zeros((pix_rows, pix_cols), jnp.float32), unroll=16)
    out_ref[...] = acc


def image(receivers, waves, delays):
    pairs, pix_rows, pix_cols = delays.shape
    return pl.pallas_call(
        image_kernel,
        out_shape=jax.ShapeDtypeStruct((pix_rows, pix_cols), jnp.float32),
        in_specs=[
            pl.BlockSpec(memory_space=pltpu.SMEM),
            pl.BlockSpec(memory_space=pltpu.VMEM),
            pl.BlockSpec(memory_space=pltpu.VMEM),
        ],
        out_specs=pl.BlockSpec(memory_space=pltpu.VMEM),
        cost_estimate=pl.CostEstimate(
            flops=8 * pairs * pix_rows * pix_cols,
            bytes_accessed=4 * (waves.size + delays.size + pix_rows * pix_cols),
            transcendentals=0,
        ),
    )(receivers, waves, delays)


def a2a_gather(block, axes, count):
    spread = jnp.broadcast_to(block[None], (count,) + block.shape)
    gathered = lax.all_to_all(spread, axes, 0, 0, tiled=True)
    return gathered.reshape((-1,) + block.shape[1:])


def gather_waves(local_waves):
    inner_waves = a2a_gather(local_waves, "hoop", lax.axis_size("hoop"))
    return a2a_gather(inner_waves, "axial", lax.axis_size("axial"))


def per_device(wave_state, layup_zone, moduli, sensors, history, receivers, delays):
    rows, cols = layup_zone.shape
    na = lax.axis_size("axial")
    stacked = jnp.concatenate(
        [wave_state[0], layup_zone.astype(jnp.float32)[None]], axis=0
    )
    hist = history[0]
    hist_count = hist.shape[1]
    hist_wide = jnp.concatenate(
        [hist, jnp.zeros((hist.shape[0], STEPS), jnp.float32)], axis=1
    )
    hoop_count = lax.axis_size("hoop")
    hist_wide = jnp.broadcast_to(hist_wide[None], (hoop_count,) + hist_wide.shape)
    cell = lax.broadcasted_iota(jnp.int32, (sensors.shape[0], rows * cols), 1)
    hit = cell == sensors[:, None]
    stacked, hist_wide, hit = lax.optimization_barrier((stacked, hist_wide, hit))
    padded = exchange(stacked, HALO)
    zone = padded[5].astype(jnp.int32)
    global_row = lax.axis_index("axial") * rows - HALO + lax.broadcasted_iota(
        jnp.int32, zone.shape, 0
    )
    inside = (global_row >= 0) & (global_row < na * rows)
    moduli_map = jnp.zeros((moduli.shape[1],) + zone.shape, jnp.float32)
    for zone_level in range(moduli.shape[0]):
        moduli_map = jnp.where(
            (zone == zone_level)[None], moduli[zone_level][:, None, None], moduli_map
        )
    moduli_map = jnp.where(inside[None], moduli_map, jnp.float32(0.0))
    fields = tuple(padded[c] for c in range(5))
    samples = []
    for step_index in range(STEPS):
        fields, moduli_map = advance(fields, moduli_map)
        moduli_map = [inner(m) for m in moduli_map]
        off = HALO - 2 * (step_index + 1)
        total = fields[2] + fields[3]
        tile = total[off:off + rows, off:off + cols]
        flat = tile.reshape(1, -1)
        samples.append(jnp.sum(jnp.where(hit, flat, jnp.float32(0.0)), axis=1))
        moduli_map = jnp.stack(moduli_map)
    next_state = jnp.stack(fields)[None]
    recorded = jnp.stack(samples, axis=1)[None]
    column = lax.broadcasted_iota(jnp.int32, hist_wide.shape, hist_wide.ndim - 1)
    trace_wide = jnp.pad(recorded[0], ((0, 0), (hist_count, 0)))
    spread = jnp.where(column >= hist_count, trace_wide[None], hist_wide)
    inner_waves = lax.all_to_all(spread, "hoop", 0, 0, tiled=True).reshape(
        (-1,) + spread.shape[2:]
    )
    waveforms = a2a_gather(inner_waves, "axial", lax.axis_size("axial"))
    partial_value = image(receivers[0], waveforms, delays[0])
    parts = lax.all_gather(partial_value.reshape(-1), "act").reshape((-1,) + partial_value.shape)
    summed = parts[0]
    for a in range(1, parts.shape[0]):
        summed = summed + parts[a]
    damage_map = summed * summed / (receivers.shape[1] * lax.axis_size("act"))
    return (next_state, recorded, damage_map)


def solution(mesh):
    return jax.shard_map(
        per_device,
        mesh=mesh,
        in_specs=(
            P("act", None, "axial", "hoop"),
            P("axial", "hoop"),
            P(),
            P(("axial", "hoop")),
            P("act", ("axial", "hoop"), None),
            P("act", None),
            P("act", None, "axial", "hoop"),
        ),
        out_specs=(
            P("act", None, "axial", "hoop"),
            P("act", ("axial", "hoop"), None),
            P("axial", "hoop"),
        ),
        check_vma=False,
    )
```

```python
import functools

import jax
import jax.numpy as jnp
from jax import lax
from jax.experimental import pallas as pl
from jax.experimental.pallas import tpu as pltpu
from jax.sharding import PartitionSpec as P

STEPS = 3
HALO = 2 * STEPS


def exchange(cells, halo):
    na = lax.axis_size("axial")
    nh = lax.axis_size("hoop")
    from_left = lax.ppermute(cells[:, :, -halo:], "hoop", [(j, (j + 1) % nh) for j in range(nh)])
    from_right = lax.ppermute(cells[:, :, :halo], "hoop", [((j + 1) % nh, j) for j in range(nh)])
    cells = jnp.concatenate([from_left, cells, from_right], axis=2)
    from_above = lax.ppermute(cells[:, -halo:, :], "axial", [(i, i + 1) for i in range(na - 1)])
    from_below = lax.ppermute(cells[:, :halo, :], "axial", [(i + 1, i) for i in range(na - 1)])
    return jnp.concatenate([from_above, cells, from_below], axis=1)


def inner(f):
    return f[1:-1, 1:-1]


def advance(fields, moduli_map):
    speed_axial, speed_hoop, normal_axial, normal_hoop, shear_stress = fields
    m = [inner(moduli_map[i]) for i in range(6)]
    mobility_axial, mobility_hoop = m[0], m[1]
    na_c = inner(normal_axial)
    nh_c = inner(normal_hoop)
    ss_c = inner(shear_stress)
    speed_axial = inner(speed_axial) + mobility_axial * (
        (normal_axial[2:, 1:-1] - na_c) + (ss_c - shear_stress[1:-1, :-2])
    )
    speed_hoop = inner(speed_hoop) + mobility_hoop * (
        (normal_hoop[1:-1, 2:] - nh_c) + (ss_c - shear_stress[:-2, 1:-1])
    )
    stiff_axial, stiff_cross, stiff_hoop, stiff_shear = (inner(m[i]) for i in range(2, 6))
    va_c = inner(speed_axial)
    vh_c = inner(speed_hoop)
    strain_axial = va_c - speed_axial[:-2, 1:-1]
    strain_hoop = vh_c - speed_hoop[1:-1, :-2]
    normal_axial = inner(na_c) + stiff_axial * strain_axial + stiff_cross * strain_hoop
    normal_hoop = inner(nh_c) + stiff_cross * strain_axial + stiff_hoop * strain_hoop
    strain_shear = (speed_axial[1:-1, 2:] - va_c) + (speed_hoop[2:, 1:-1] - vh_c)
    shear_stress = inner(ss_c) + stiff_shear * strain_shear
    return (va_c, vh_c, normal_axial, normal_hoop, shear_stress), m


def image_kernel(receivers_ref, waves_ref, delays_ref, out_ref):
    pairs, pix_rows, pix_cols = delays_ref.shape
    lanes = pix_cols
    tile = 8

    def body(k, acc):
        row = receivers_ref[k]
        base = pl.multiple_of((row // tile) * tile, tile)
        block = waves_ref[pl.ds(base, tile), :]
        pick = jnp.full(block.shape, row % tile, jnp.int32)
        spread = jnp.take_along_axis(block, pick, axis=0, mode="promise_in_bounds")
        low = spread[:, :lanes]
        high = spread[:, lanes:]
        parts = []
        for h in range(pix_rows // tile):
            d = delays_ref[k, pl.ds(h * tile, tile), :]
            idx = d & (lanes - 1)
            got_low = jnp.take_along_axis(low, idx, axis=1, mode="promise_in_bounds")
            got_high = jnp.take_along_axis(high, idx, axis=1, mode="promise_in_bounds")
            parts.append(jnp.where(d >= lanes, got_high, got_low))
        return acc + jnp.concatenate(parts, axis=0)

    acc = lax.fori_loop(0, pairs, body, jnp.zeros((pix_rows, pix_cols), jnp.float32), unroll=16)
    out_ref[...] = acc


def image(receivers, waves, delays):
    pairs, pix_rows, pix_cols = delays.shape
    return pl.pallas_call(
        image_kernel,
        out_shape=jax.ShapeDtypeStruct((pix_rows, pix_cols), jnp.float32),
        in_specs=[
            pl.BlockSpec(memory_space=pltpu.SMEM),
            pl.BlockSpec(memory_space=pltpu.VMEM),
            pl.BlockSpec(memory_space=pltpu.VMEM),
        ],
        out_specs=pl.BlockSpec(memory_space=pltpu.VMEM),
        cost_estimate=pl.CostEstimate(
            flops=8 * pairs * pix_rows * pix_cols,
            bytes_accessed=4 * (waves.size + delays.size + pix_rows * pix_cols),
            transcendentals=0,
        ),
    )(receivers, waves, delays)


def a2a_gather(block, axes, count):
    spread = jnp.broadcast_to(block[None], (count,) + block.shape)
    gathered = lax.all_to_all(spread, axes, 0, 0, tiled=True)
    return gathered.reshape((-1,) + block.shape[1:])


def gather_waves(local_waves):
    inner_waves = a2a_gather(local_waves, "hoop", lax.axis_size("hoop"))
    return a2a_gather(inner_waves, "axial", lax.axis_size("axial"))


def per_device(wave_state, layup_zone, moduli, sensors, history, receivers, delays):
    rows, cols = layup_zone.shape
    na = lax.axis_size("axial")
    local_moduli = jnp.zeros((moduli.shape[1],) + layup_zone.shape, jnp.float32)
    for zone_level in range(moduli.shape[0]):
        local_moduli = jnp.where(
            (layup_zone == zone_level)[None], moduli[zone_level][:, None, None], local_moduli
        )
    stacked = jnp.concatenate([wave_state[0], local_moduli], axis=0)
    hist = history[0]
    hist_count = hist.shape[1]
    hist_wide = jnp.concatenate(
        [hist, jnp.zeros((hist.shape[0], STEPS), jnp.float32)], axis=1
    )
    hoop_count = lax.axis_size("hoop")
    hist_wide = jnp.broadcast_to(hist_wide[None], (hoop_count,) + hist_wide.shape)
    cell = lax.broadcasted_iota(jnp.int32, (sensors.shape[0], rows * cols), 1)
    hit = cell == sensors[:, None]
    stacked, hist_wide, hit = lax.optimization_barrier((stacked, hist_wide, hit))
    padded = exchange(stacked, HALO)
    moduli_map = padded[5:]
    fields = tuple(padded[c] for c in range(5))
    samples = []
    for step_index in range(STEPS):
        fields, moduli_map = advance(fields, moduli_map)
        moduli_map = [inner(m) for m in moduli_map]
        off = HALO - 2 * (step_index + 1)
        total = fields[2] + fields[3]
        tile = total[off:off + rows, off:off + cols]
        flat = tile.reshape(1, -1)
        samples.append(jnp.sum(jnp.where(hit, flat, jnp.float32(0.0)), axis=1))
        moduli_map = jnp.stack(moduli_map)
    next_state = jnp.stack(fields)[None]
    recorded = jnp.stack(samples, axis=1)[None]
    column = lax.broadcasted_iota(jnp.int32, hist_wide.shape, hist_wide.ndim - 1)
    trace_wide = jnp.pad(recorded[0], ((0, 0), (hist_count, 0)))
    spread = jnp.where(column >= hist_count, trace_wide[None], hist_wide)
    inner_waves = lax.all_to_all(spread, "hoop", 0, 0, tiled=True).reshape(
        (-1,) + spread.shape[2:]
    )
    waveforms = a2a_gather(inner_waves, "axial", lax.axis_size("axial"))
    partial_value = image(receivers[0], waveforms, delays[0])
    parts = lax.all_gather(partial_value.reshape(-1), "act").reshape((-1,) + partial_value.shape)
    summed = parts[0]
    for a in range(1, parts.shape[0]):
        summed = summed + parts[a]
    damage_map = summed * summed / (receivers.shape[1] * lax.axis_size("act"))
    return (next_state, recorded, damage_map)


def solution(mesh):
    return jax.shard_map(
        per_device,
        mesh=mesh,
        in_specs=(
            P("act", None, "axial", "hoop"),
            P("axial", "hoop"),
            P(),
            P(("axial", "hoop")),
            P("act", ("axial", "hoop"), None),
            P("act", None),
            P("act", None, "axial", "hoop"),
        ),
        out_specs=(
            P("act", None, "axial", "hoop"),
            P("act", ("axial", "hoop"), None),
            P("axial", "hoop"),
        ),
        check_vma=False,
    )
```

```python
import functools

import jax
import jax.numpy as jnp
from jax import lax
from jax.experimental import pallas as pl
from jax.experimental.pallas import tpu as pltpu
from jax.sharding import PartitionSpec as P

STEPS = 3
HALO = 2 * STEPS


def exchange(cells, halo):
    na = lax.axis_size("axial")
    nh = lax.axis_size("hoop")
    from_left = lax.ppermute(cells[:, :, -halo:], "hoop", [(j, (j + 1) % nh) for j in range(nh)])
    from_right = lax.ppermute(cells[:, :, :halo], "hoop", [((j + 1) % nh, j) for j in range(nh)])
    cells = jnp.concatenate([from_left, cells, from_right], axis=2)
    from_above = lax.ppermute(cells[:, -halo:, :], "axial", [(i, i + 1) for i in range(na - 1)])
    from_below = lax.ppermute(cells[:, :halo, :], "axial", [(i + 1, i) for i in range(na - 1)])
    return jnp.concatenate([from_above, cells, from_below], axis=1)


def inner(f):
    return f[1:-1, 1:-1]


def advance(fields, moduli_map):
    speed_axial, speed_hoop, normal_axial, normal_hoop, shear_stress = fields
    m = [inner(moduli_map[i]) for i in range(6)]
    mobility_axial, mobility_hoop = m[0], m[1]
    na_c = inner(normal_axial)
    nh_c = inner(normal_hoop)
    ss_c = inner(shear_stress)
    speed_axial = inner(speed_axial) + mobility_axial * (
        (normal_axial[2:, 1:-1] - na_c) + (ss_c - shear_stress[1:-1, :-2])
    )
    speed_hoop = inner(speed_hoop) + mobility_hoop * (
        (normal_hoop[1:-1, 2:] - nh_c) + (ss_c - shear_stress[:-2, 1:-1])
    )
    stiff_axial, stiff_cross, stiff_hoop, stiff_shear = (inner(m[i]) for i in range(2, 6))
    va_c = inner(speed_axial)
    vh_c = inner(speed_hoop)
    strain_axial = va_c - speed_axial[:-2, 1:-1]
    strain_hoop = vh_c - speed_hoop[1:-1, :-2]
    normal_axial = inner(na_c) + stiff_axial * strain_axial + stiff_cross * strain_hoop
    normal_hoop = inner(nh_c) + stiff_cross * strain_axial + stiff_hoop * strain_hoop
    strain_shear = (speed_axial[1:-1, 2:] - va_c) + (speed_hoop[2:, 1:-1] - vh_c)
    shear_stress = inner(ss_c) + stiff_shear * strain_shear
    return (va_c, vh_c, normal_axial, normal_hoop, shear_stress), m


def image_kernel(receivers_ref, waves_ref, delays_ref, out_ref):
    pairs, pix_rows, pix_cols = delays_ref.shape
    lanes = pix_cols
    tile = 8

    def body(k, acc):
        row = receivers_ref[k]
        base = pl.multiple_of((row // tile) * tile, tile)
        block = waves_ref[pl.ds(base, tile), :]
        pick = jnp.full(block.shape, row % tile, jnp.int32)
        spread = jnp.take_along_axis(block, pick, axis=0, mode="promise_in_bounds")
        low = spread[:, :lanes]
        high = spread[:, lanes:]
        parts = []
        for h in range(pix_rows // tile):
            d = delays_ref[k, pl.ds(h * tile, tile), :]
            idx = d & (lanes - 1)
            got_low = jnp.take_along_axis(low, idx, axis=1, mode="promise_in_bounds")
            got_high = jnp.take_along_axis(high, idx, axis=1, mode="promise_in_bounds")
            parts.append(jnp.where(d >= lanes, got_high, got_low))
        return acc + jnp.concatenate(parts, axis=0)

    acc = lax.fori_loop(0, pairs, body, jnp.zeros((pix_rows, pix_cols), jnp.float32), unroll=32)
    out_ref[...] = acc


def image(receivers, waves, delays):
    pairs, pix_rows, pix_cols = delays.shape
    return pl.pallas_call(
        image_kernel,
        out_shape=jax.ShapeDtypeStruct((pix_rows, pix_cols), jnp.float32),
        in_specs=[
            pl.BlockSpec(memory_space=pltpu.SMEM),
            pl.BlockSpec(memory_space=pltpu.VMEM),
            pl.BlockSpec(memory_space=pltpu.VMEM),
        ],
        out_specs=pl.BlockSpec(memory_space=pltpu.VMEM),
        cost_estimate=pl.CostEstimate(
            flops=8 * pairs * pix_rows * pix_cols,
            bytes_accessed=4 * (waves.size + delays.size + pix_rows * pix_cols),
            transcendentals=0,
        ),
    )(receivers, waves, delays)


def a2a_gather(block, axes, count):
    spread = jnp.broadcast_to(block[None], (count,) + block.shape)
    gathered = lax.all_to_all(spread, axes, 0, 0, tiled=True)
    return gathered.reshape((-1,) + block.shape[1:])


def gather_waves(local_waves):
    inner_waves = a2a_gather(local_waves, "hoop", lax.axis_size("hoop"))
    return a2a_gather(inner_waves, "axial", lax.axis_size("axial"))


def per_device(wave_state, layup_zone, moduli, sensors, history, receivers, delays):
    rows, cols = layup_zone.shape
    na = lax.axis_size("axial")
    stacked = jnp.concatenate(
        [wave_state[0], layup_zone.astype(jnp.float32)[None]], axis=0
    )
    hist = history[0]
    hist_count = hist.shape[1]
    hist_wide = jnp.concatenate(
        [hist, jnp.zeros((hist.shape[0], STEPS), jnp.float32)], axis=1
    )
    hoop_count = lax.axis_size("hoop")
    hist_wide = jnp.broadcast_to(hist_wide[None], (hoop_count,) + hist_wide.shape)
    cell = lax.broadcasted_iota(jnp.int32, (sensors.shape[0], rows * cols), 1)
    hit = cell == sensors[:, None]
    stacked, hist_wide, hit = lax.optimization_barrier((stacked, hist_wide, hit))
    padded = exchange(stacked, HALO)
    zone = padded[5].astype(jnp.int32)
    global_row = lax.axis_index("axial") * rows - HALO + lax.broadcasted_iota(
        jnp.int32, zone.shape, 0
    )
    inside = (global_row >= 0) & (global_row < na * rows)
    moduli_map = jnp.zeros((moduli.shape[1],) + zone.shape, jnp.float32)
    for zone_level in range(moduli.shape[0]):
        moduli_map = jnp.where(
            (zone == zone_level)[None], moduli[zone_level][:, None, None], moduli_map
        )
    moduli_map = jnp.where(inside[None], moduli_map, jnp.float32(0.0))
    fields = tuple(padded[c] for c in range(5))
    samples = []
    for step_index in range(STEPS):
        fields, moduli_map = advance(fields, moduli_map)
        moduli_map = [inner(m) for m in moduli_map]
        off = HALO - 2 * (step_index + 1)
        total = fields[2] + fields[3]
        tile = total[off:off + rows, off:off + cols]
        flat = tile.reshape(1, -1)
        samples.append(jnp.sum(jnp.where(hit, flat, jnp.float32(0.0)), axis=1))
        moduli_map = jnp.stack(moduli_map)
    next_state = jnp.stack(fields)[None]
    recorded = jnp.stack(samples, axis=1)[None]
    column = lax.broadcasted_iota(jnp.int32, hist_wide.shape, hist_wide.ndim - 1)
    trace_wide = jnp.pad(recorded[0], ((0, 0), (hist_count, 0)))
    spread = jnp.where(column >= hist_count, trace_wide[None], hist_wide)
    inner_waves = lax.all_to_all(spread, "hoop", 0, 0, tiled=True).reshape(
        (-1,) + spread.shape[2:]
    )
    waveforms = a2a_gather(inner_waves, "axial", lax.axis_size("axial"))
    partial_value = image(receivers[0], waveforms, delays[0])
    parts = lax.all_gather(partial_value.reshape(-1), "act").reshape((-1,) + partial_value.shape)
    summed = parts[0]
    for a in range(1, parts.shape[0]):
        summed = summed + parts[a]
    damage_map = summed * summed / (receivers.shape[1] * lax.axis_size("act"))
    return (next_state, recorded, damage_map)


def solution(mesh):
    return jax.shard_map(
        per_device,
        mesh=mesh,
        in_specs=(
            P("act", None, "axial", "hoop"),
            P("axial", "hoop"),
            P(),
            P(("axial", "hoop")),
            P("act", ("axial", "hoop"), None),
            P("act", None),
            P("act", None, "axial", "hoop"),
        ),
        out_specs=(
            P("act", None, "axial", "hoop"),
            P("act", ("axial", "hoop"), None),
            P("axial", "hoop"),
        ),
        check_vma=False,
    )
```

```python
import functools

import jax
import jax.numpy as jnp
from jax import lax
from jax.experimental import pallas as pl
from jax.experimental.pallas import tpu as pltpu
from jax.sharding import PartitionSpec as P

STEPS = 3
HALO = 2 * STEPS


def exchange(cells, halo):
    na = lax.axis_size("axial")
    nh = lax.axis_size("hoop")
    from_left = lax.ppermute(cells[:, :, -halo:], "hoop", [(j, (j + 1) % nh) for j in range(nh)])
    from_right = lax.ppermute(cells[:, :, :halo], "hoop", [((j + 1) % nh, j) for j in range(nh)])
    cells = jnp.concatenate([from_left, cells, from_right], axis=2)
    from_above = lax.ppermute(cells[:, -halo:, :], "axial", [(i, i + 1) for i in range(na - 1)])
    from_below = lax.ppermute(cells[:, :halo, :], "axial", [(i + 1, i) for i in range(na - 1)])
    return jnp.concatenate([from_above, cells, from_below], axis=1)


def inner(f):
    return f[1:-1, 1:-1]


def advance(fields, moduli_map):
    speed_axial, speed_hoop, normal_axial, normal_hoop, shear_stress = fields
    m = [inner(moduli_map[i]) for i in range(6)]
    mobility_axial, mobility_hoop = m[0], m[1]
    na_c = inner(normal_axial)
    nh_c = inner(normal_hoop)
    ss_c = inner(shear_stress)
    speed_axial = inner(speed_axial) + mobility_axial * (
        (normal_axial[2:, 1:-1] - na_c) + (ss_c - shear_stress[1:-1, :-2])
    )
    speed_hoop = inner(speed_hoop) + mobility_hoop * (
        (normal_hoop[1:-1, 2:] - nh_c) + (ss_c - shear_stress[:-2, 1:-1])
    )
    stiff_axial, stiff_cross, stiff_hoop, stiff_shear = (inner(m[i]) for i in range(2, 6))
    va_c = inner(speed_axial)
    vh_c = inner(speed_hoop)
    strain_axial = va_c - speed_axial[:-2, 1:-1]
    strain_hoop = vh_c - speed_hoop[1:-1, :-2]
    normal_axial = inner(na_c) + stiff_axial * strain_axial + stiff_cross * strain_hoop
    normal_hoop = inner(nh_c) + stiff_cross * strain_axial + stiff_hoop * strain_hoop
    strain_shear = (speed_axial[1:-1, 2:] - va_c) + (speed_hoop[2:, 1:-1] - vh_c)
    shear_stress = inner(ss_c) + stiff_shear * strain_shear
    return (va_c, vh_c, normal_axial, normal_hoop, shear_stress), m


def image_kernel(receivers_ref, waves_ref, delays_ref, out_ref):
    pairs, pix_rows, pix_cols = delays_ref.shape
    lanes = pix_cols
    tile = 8

    def body(k, acc):
        row = receivers_ref[k]
        base = pl.multiple_of((row // tile) * tile, tile)
        block = waves_ref[pl.ds(base, tile), :]
        pick = jnp.full(block.shape, row % tile, jnp.int32)
        spread = jnp.take_along_axis(block, pick, axis=0, mode="promise_in_bounds")
        low = spread[:, :lanes]
        high = spread[:, lanes:]
        parts = []
        for h in range(pix_rows // tile):
            d = delays_ref[k, pl.ds(h * tile, tile), :]
            idx = d & (lanes - 1)
            got_low = jnp.take_along_axis(low, idx, axis=1, mode="promise_in_bounds")
            got_high = jnp.take_along_axis(high, idx, axis=1, mode="promise_in_bounds")
            parts.append(jnp.where(d >= lanes, got_high, got_low))
        return acc + jnp.concatenate(parts, axis=0)

    acc = lax.fori_loop(0, pairs, body, jnp.zeros((pix_rows, pix_cols), jnp.float32), unroll=64)
    out_ref[...] = acc


def image(receivers, waves, delays):
    pairs, pix_rows, pix_cols = delays.shape
    return pl.pallas_call(
        image_kernel,
        out_shape=jax.ShapeDtypeStruct((pix_rows, pix_cols), jnp.float32),
        in_specs=[
            pl.BlockSpec(memory_space=pltpu.SMEM),
            pl.BlockSpec(memory_space=pltpu.VMEM),
            pl.BlockSpec(memory_space=pltpu.VMEM),
        ],
        out_specs=pl.BlockSpec(memory_space=pltpu.VMEM),
        cost_estimate=pl.CostEstimate(
            flops=8 * pairs * pix_rows * pix_cols,
            bytes_accessed=4 * (waves.size + delays.size + pix_rows * pix_cols),
            transcendentals=0,
        ),
    )(receivers, waves, delays)


def a2a_gather(block, axes, count):
    spread = jnp.broadcast_to(block[None], (count,) + block.shape)
    gathered = lax.all_to_all(spread, axes, 0, 0, tiled=True)
    return gathered.reshape((-1,) + block.shape[1:])


def gather_waves(local_waves):
    inner_waves = a2a_gather(local_waves, "hoop", lax.axis_size("hoop"))
    return a2a_gather(inner_waves, "axial", lax.axis_size("axial"))


def per_device(wave_state, layup_zone, moduli, sensors, history, receivers, delays):
    rows, cols = layup_zone.shape
    na = lax.axis_size("axial")
    stacked = jnp.concatenate(
        [wave_state[0], layup_zone.astype(jnp.float32)[None]], axis=0
    )
    hist = history[0]
    hist_count = hist.shape[1]
    hist_wide = jnp.concatenate(
        [hist, jnp.zeros((hist.shape[0], STEPS), jnp.float32)], axis=1
    )
    hoop_count = lax.axis_size("hoop")
    hist_wide = jnp.broadcast_to(hist_wide[None], (hoop_count,) + hist_wide.shape)
    cell = lax.broadcasted_iota(jnp.int32, (sensors.shape[0], rows * cols), 1)
    hit = cell == sensors[:, None]
    stacked, hist_wide, hit = lax.optimization_barrier((stacked, hist_wide, hit))
    padded = exchange(stacked, HALO)
    zone = padded[5].astype(jnp.int32)
    global_row = lax.axis_index("axial") * rows - HALO + lax.broadcasted_iota(
        jnp.int32, zone.shape, 0
    )
    inside = (global_row >= 0) & (global_row < na * rows)
    moduli_map = jnp.zeros((moduli.shape[1],) + zone.shape, jnp.float32)
    for zone_level in range(moduli.shape[0]):
        moduli_map = jnp.where(
            (zone == zone_level)[None], moduli[zone_level][:, None, None], moduli_map
        )
    moduli_map = jnp.where(inside[None], moduli_map, jnp.float32(0.0))
    fields = tuple(padded[c] for c in range(5))
    samples = []
    for step_index in range(STEPS):
        fields, moduli_map = advance(fields, moduli_map)
        moduli_map = [inner(m) for m in moduli_map]
        off = HALO - 2 * (step_index + 1)
        total = fields[2] + fields[3]
        tile = total[off:off + rows, off:off + cols]
        flat = tile.reshape(1, -1)
        samples.append(jnp.sum(jnp.where(hit, flat, jnp.float32(0.0)), axis=1))
        moduli_map = jnp.stack(moduli_map)
    next_state = jnp.stack(fields)[None]
    recorded = jnp.stack(samples, axis=1)[None]
    column = lax.broadcasted_iota(jnp.int32, hist_wide.shape, hist_wide.ndim - 1)
    trace_wide = jnp.pad(recorded[0], ((0, 0), (hist_count, 0)))
    spread = jnp.where(column >= hist_count, trace_wide[None], hist_wide)
    inner_waves = lax.all_to_all(spread, "hoop", 0, 0, tiled=True).reshape(
        (-1,) + spread.shape[2:]
    )
    waveforms = a2a_gather(inner_waves, "axial", lax.axis_size("axial"))
    partial_value = image(receivers[0], waveforms, delays[0])
    parts = lax.all_gather(partial_value.reshape(-1), "act").reshape((-1,) + partial_value.shape)
    summed = parts[0]
    for a in range(1, parts.shape[0]):
        summed = summed + parts[a]
    damage_map = summed * summed / (receivers.shape[1] * lax.axis_size("act"))
    return (next_state, recorded, damage_map)


def solution(mesh):
    return jax.shard_map(
        per_device,
        mesh=mesh,
        in_specs=(
            P("act", None, "axial", "hoop"),
            P("axial", "hoop"),
            P(),
            P(("axial", "hoop")),
            P("act", ("axial", "hoop"), None),
            P("act", None),
            P("act", None, "axial", "hoop"),
        ),
        out_specs=(
            P("act", None, "axial", "hoop"),
            P("act", ("axial", "hoop"), None),
            P("axial", "hoop"),
        ),
        check_vma=False,
    )
```

```python
import functools

import jax
import jax.numpy as jnp
from jax import lax
from jax.experimental import pallas as pl
from jax.experimental.pallas import tpu as pltpu
from jax.sharding import PartitionSpec as P

STEPS = 3
HALO = 2 * STEPS


def exchange(cells, halo):
    na = lax.axis_size("axial")
    nh = lax.axis_size("hoop")
    from_left = lax.ppermute(cells[:, :, -halo:], "hoop", [(j, (j + 1) % nh) for j in range(nh)])
    from_right = lax.ppermute(cells[:, :, :halo], "hoop", [((j + 1) % nh, j) for j in range(nh)])
    cells = jnp.concatenate([from_left, cells, from_right], axis=2)
    from_above = lax.ppermute(cells[:, -halo:, :], "axial", [(i, i + 1) for i in range(na - 1)])
    from_below = lax.ppermute(cells[:, :halo, :], "axial", [(i + 1, i) for i in range(na - 1)])
    return jnp.concatenate([from_above, cells, from_below], axis=1)


def inner(f):
    return f[1:-1, 1:-1]


def advance(fields, moduli_map):
    speed_axial, speed_hoop, normal_axial, normal_hoop, shear_stress = fields
    m = [inner(moduli_map[i]) for i in range(6)]
    mobility_axial, mobility_hoop = m[0], m[1]
    na_c = inner(normal_axial)
    nh_c = inner(normal_hoop)
    ss_c = inner(shear_stress)
    speed_axial = inner(speed_axial) + mobility_axial * (
        (normal_axial[2:, 1:-1] - na_c) + (ss_c - shear_stress[1:-1, :-2])
    )
    speed_hoop = inner(speed_hoop) + mobility_hoop * (
        (normal_hoop[1:-1, 2:] - nh_c) + (ss_c - shear_stress[:-2, 1:-1])
    )
    stiff_axial, stiff_cross, stiff_hoop, stiff_shear = (inner(m[i]) for i in range(2, 6))
    va_c = inner(speed_axial)
    vh_c = inner(speed_hoop)
    strain_axial = va_c - speed_axial[:-2, 1:-1]
    strain_hoop = vh_c - speed_hoop[1:-1, :-2]
    normal_axial = inner(na_c) + stiff_axial * strain_axial + stiff_cross * strain_hoop
    normal_hoop = inner(nh_c) + stiff_cross * strain_axial + stiff_hoop * strain_hoop
    strain_shear = (speed_axial[1:-1, 2:] - va_c) + (speed_hoop[2:, 1:-1] - vh_c)
    shear_stress = inner(ss_c) + stiff_shear * strain_shear
    return (va_c, vh_c, normal_axial, normal_hoop, shear_stress), m


def image_kernel(receivers_ref, waves_ref, delays_ref, out_ref):
    pairs, pix_rows, pix_cols = delays_ref.shape
    lanes = pix_cols
    tile = 8

    def body(k, acc):
        row = receivers_ref[k]
        base = pl.multiple_of((row // tile) * tile, tile)
        block = waves_ref[pl.ds(base, tile), :]
        pick = jnp.full(block.shape, row % tile, jnp.int32)
        spread = jnp.take_along_axis(block, pick, axis=0, mode="promise_in_bounds")
        low = spread[:, :lanes]
        high = spread[:, lanes:]
        parts = []
        for h in range(pix_rows // tile):
            d = delays_ref[k, pl.ds(h * tile, tile), :]
            idx = d & (lanes - 1)
            got_low = jnp.take_along_axis(low, idx, axis=1, mode="promise_in_bounds")
            got_high = jnp.take_along_axis(high, idx, axis=1, mode="promise_in_bounds")
            parts.append(jnp.where(d >= lanes, got_high, got_low))
        return acc + jnp.concatenate(parts, axis=0)

    acc = lax.fori_loop(0, pairs, body, jnp.zeros((pix_rows, pix_cols), jnp.float32), unroll=True)
    out_ref[...] = acc


def image(receivers, waves, delays):
    pairs, pix_rows, pix_cols = delays.shape
    return pl.pallas_call(
        image_kernel,
        out_shape=jax.ShapeDtypeStruct((pix_rows, pix_cols), jnp.float32),
        in_specs=[
            pl.BlockSpec(memory_space=pltpu.SMEM),
            pl.BlockSpec(memory_space=pltpu.VMEM),
            pl.BlockSpec(memory_space=pltpu.VMEM),
        ],
        out_specs=pl.BlockSpec(memory_space=pltpu.VMEM),
        cost_estimate=pl.CostEstimate(
            flops=8 * pairs * pix_rows * pix_cols,
            bytes_accessed=4 * (waves.size + delays.size + pix_rows * pix_cols),
            transcendentals=0,
        ),
    )(receivers, waves, delays)


def a2a_gather(block, axes, count):
    spread = jnp.broadcast_to(block[None], (count,) + block.shape)
    gathered = lax.all_to_all(spread, axes, 0, 0, tiled=True)
    return gathered.reshape((-1,) + block.shape[1:])


def gather_waves(local_waves):
    inner_waves = a2a_gather(local_waves, "hoop", lax.axis_size("hoop"))
    return a2a_gather(inner_waves, "axial", lax.axis_size("axial"))


def per_device(wave_state, layup_zone, moduli, sensors, history, receivers, delays):
    rows, cols = layup_zone.shape
    na = lax.axis_size("axial")
    stacked = jnp.concatenate(
        [wave_state[0], layup_zone.astype(jnp.float32)[None]], axis=0
    )
    hist = history[0]
    hist_count = hist.shape[1]
    hist_wide = jnp.concatenate(
        [hist, jnp.zeros((hist.shape[0], STEPS), jnp.float32)], axis=1
    )
    hoop_count = lax.axis_size("hoop")
    hist_wide = jnp.broadcast_to(hist_wide[None], (hoop_count,) + hist_wide.shape)
    cell = lax.broadcasted_iota(jnp.int32, (sensors.shape[0], rows * cols), 1)
    hit = cell == sensors[:, None]
    stacked, hist_wide, hit = lax.optimization_barrier((stacked, hist_wide, hit))
    padded = exchange(stacked, HALO)
    zone = padded[5].astype(jnp.int32)
    global_row = lax.axis_index("axial") * rows - HALO + lax.broadcasted_iota(
        jnp.int32, zone.shape, 0
    )
    inside = (global_row >= 0) & (global_row < na * rows)
    moduli_map = jnp.zeros((moduli.shape[1],) + zone.shape, jnp.float32)
    for zone_level in range(moduli.shape[0]):
        moduli_map = jnp.where(
            (zone == zone_level)[None], moduli[zone_level][:, None, None], moduli_map
        )
    moduli_map = jnp.where(inside[None], moduli_map, jnp.float32(0.0))
    fields = tuple(padded[c] for c in range(5))
    samples = []
    for step_index in range(STEPS):
        fields, moduli_map = advance(fields, moduli_map)
        moduli_map = [inner(m) for m in moduli_map]
        off = HALO - 2 * (step_index + 1)
        total = fields[2] + fields[3]
        tile = total[off:off + rows, off:off + cols]
        flat = tile.reshape(1, -1)
        samples.append(jnp.sum(jnp.where(hit, flat, jnp.float32(0.0)), axis=1))
        moduli_map = jnp.stack(moduli_map)
    next_state = jnp.stack(fields)[None]
    recorded = jnp.stack(samples, axis=1)[None]
    column = lax.broadcasted_iota(jnp.int32, hist_wide.shape, hist_wide.ndim - 1)
    trace_wide = jnp.pad(recorded[0], ((0, 0), (hist_count, 0)))
    spread = jnp.where(column >= hist_count, trace_wide[None], hist_wide)
    inner_waves = lax.all_to_all(spread, "hoop", 0, 0, tiled=True).reshape(
        (-1,) + spread.shape[2:]
    )
    waveforms = a2a_gather(inner_waves, "axial", lax.axis_size("axial"))
    partial_value = image(receivers[0], waveforms, delays[0])
    parts = lax.all_gather(partial_value.reshape(-1), "act").reshape((-1,) + partial_value.shape)
    summed = parts[0]
    for a in range(1, parts.shape[0]):
        summed = summed + parts[a]
    damage_map = summed * summed / (receivers.shape[1] * lax.axis_size("act"))
    return (next_state, recorded, damage_map)


def solution(mesh):
    return jax.shard_map(
        per_device,
        mesh=mesh,
        in_specs=(
            P("act", None, "axial", "hoop"),
            P("axial", "hoop"),
            P(),
            P(("axial", "hoop")),
            P("act", ("axial", "hoop"), None),
            P("act", None),
            P("act", None, "axial", "hoop"),
        ),
        out_specs=(
            P("act", None, "axial", "hoop"),
            P("act", ("axial", "hoop"), None),
            P("axial", "hoop"),
        ),
        check_vma=False,
    )
```

```python
import functools

import jax
import jax.numpy as jnp
from jax import lax
from jax.experimental import pallas as pl
from jax.experimental.pallas import tpu as pltpu
from jax.sharding import PartitionSpec as P

STEPS = 3
HALO = 2 * STEPS


def exchange(cells, halo):
    na = lax.axis_size("axial")
    nh = lax.axis_size("hoop")
    from_left = lax.ppermute(cells[:, :, -halo:], "hoop", [(j, (j + 1) % nh) for j in range(nh)])
    from_right = lax.ppermute(cells[:, :, :halo], "hoop", [((j + 1) % nh, j) for j in range(nh)])
    cells = jnp.concatenate([from_left, cells, from_right], axis=2)
    from_above = lax.ppermute(cells[:, -halo:, :], "axial", [(i, i + 1) for i in range(na - 1)])
    from_below = lax.ppermute(cells[:, :halo, :], "axial", [(i + 1, i) for i in range(na - 1)])
    return jnp.concatenate([from_above, cells, from_below], axis=1)


def inner(f):
    return f[1:-1, 1:-1]


def advance(fields, moduli_map):
    speed_axial, speed_hoop, normal_axial, normal_hoop, shear_stress = fields
    m = [inner(moduli_map[i]) for i in range(6)]
    mobility_axial, mobility_hoop = m[0], m[1]
    na_c = inner(normal_axial)
    nh_c = inner(normal_hoop)
    ss_c = inner(shear_stress)
    speed_axial = inner(speed_axial) + mobility_axial * (
        (normal_axial[2:, 1:-1] - na_c) + (ss_c - shear_stress[1:-1, :-2])
    )
    speed_hoop = inner(speed_hoop) + mobility_hoop * (
        (normal_hoop[1:-1, 2:] - nh_c) + (ss_c - shear_stress[:-2, 1:-1])
    )
    stiff_axial, stiff_cross, stiff_hoop, stiff_shear = (inner(m[i]) for i in range(2, 6))
    va_c = inner(speed_axial)
    vh_c = inner(speed_hoop)
    strain_axial = va_c - speed_axial[:-2, 1:-1]
    strain_hoop = vh_c - speed_hoop[1:-1, :-2]
    normal_axial = inner(na_c) + stiff_axial * strain_axial + stiff_cross * strain_hoop
    normal_hoop = inner(nh_c) + stiff_cross * strain_axial + stiff_hoop * strain_hoop
    strain_shear = (speed_axial[1:-1, 2:] - va_c) + (speed_hoop[2:, 1:-1] - vh_c)
    shear_stress = inner(ss_c) + stiff_shear * strain_shear
    return (va_c, vh_c, normal_axial, normal_hoop, shear_stress), m


def image_kernel(receivers_ref, waves_ref, delays_ref, out_ref):
    pairs, pix_rows, pix_cols = delays_ref.shape
    lanes = pix_cols
    tile = 8

    def body(k, acc):
        row = receivers_ref[k]
        base = pl.multiple_of((row // tile) * tile, tile)
        block = waves_ref[pl.ds(base, tile), :]
        pick = jnp.full(block.shape, row % tile, jnp.int32)
        spread = jnp.take_along_axis(block, pick, axis=0, mode="promise_in_bounds")
        low = spread[:, :lanes]
        high = spread[:, lanes:]
        parts = []
        for h in range(pix_rows // tile):
            d = delays_ref[k, pl.ds(h * tile, tile), :]
            idx = d & (lanes - 1)
            got_low = jnp.take_along_axis(low, idx, axis=1, mode="promise_in_bounds")
            got_high = jnp.take_along_axis(high, idx, axis=1, mode="promise_in_bounds")
            parts.append(jnp.where(d >= lanes, got_high, got_low))
        return acc + jnp.concatenate(parts, axis=0)

    def two(j, accs):
        return body(2 * j, accs[0]), body(2 * j + 1, accs[1])

    zero = jnp.zeros((pix_rows, pix_cols), jnp.float32)
    even, odd = lax.fori_loop(0, pairs // 2, two, (zero, zero), unroll=True)
    out_ref[...] = even + odd


def image(receivers, waves, delays):
    pairs, pix_rows, pix_cols = delays.shape
    return pl.pallas_call(
        image_kernel,
        out_shape=jax.ShapeDtypeStruct((pix_rows, pix_cols), jnp.float32),
        in_specs=[
            pl.BlockSpec(memory_space=pltpu.SMEM),
            pl.BlockSpec(memory_space=pltpu.VMEM),
            pl.BlockSpec(memory_space=pltpu.VMEM),
        ],
        out_specs=pl.BlockSpec(memory_space=pltpu.VMEM),
        cost_estimate=pl.CostEstimate(
            flops=8 * pairs * pix_rows * pix_cols,
            bytes_accessed=4 * (waves.size + delays.size + pix_rows * pix_cols),
            transcendentals=0,
        ),
    )(receivers, waves, delays)


def a2a_gather(block, axes, count):
    spread = jnp.broadcast_to(block[None], (count,) + block.shape)
    gathered = lax.all_to_all(spread, axes, 0, 0, tiled=True)
    return gathered.reshape((-1,) + block.shape[1:])


def gather_waves(local_waves):
    inner_waves = a2a_gather(local_waves, "hoop", lax.axis_size("hoop"))
    return a2a_gather(inner_waves, "axial", lax.axis_size("axial"))


def per_device(wave_state, layup_zone, moduli, sensors, history, receivers, delays):
    rows, cols = layup_zone.shape
    na = lax.axis_size("axial")
    stacked = jnp.concatenate(
        [wave_state[0], layup_zone.astype(jnp.float32)[None]], axis=0
    )
    hist = history[0]
    hist_count = hist.shape[1]
    hist_wide = jnp.concatenate(
        [hist, jnp.zeros((hist.shape[0], STEPS), jnp.float32)], axis=1
    )
    hoop_count = lax.axis_size("hoop")
    hist_wide = jnp.broadcast_to(hist_wide[None], (hoop_count,) + hist_wide.shape)
    cell = lax.broadcasted_iota(jnp.int32, (sensors.shape[0], rows * cols), 1)
    hit = cell == sensors[:, None]
    stacked, hist_wide, hit = lax.optimization_barrier((stacked, hist_wide, hit))
    padded = exchange(stacked, HALO)
    zone = padded[5].astype(jnp.int32)
    global_row = lax.axis_index("axial") * rows - HALO + lax.broadcasted_iota(
        jnp.int32, zone.shape, 0
    )
    inside = (global_row >= 0) & (global_row < na * rows)
    moduli_map = jnp.zeros((moduli.shape[1],) + zone.shape, jnp.float32)
    for zone_level in range(moduli.shape[0]):
        moduli_map = jnp.where(
            (zone == zone_level)[None], moduli[zone_level][:, None, None], moduli_map
        )
    moduli_map = jnp.where(inside[None], moduli_map, jnp.float32(0.0))
    fields = tuple(padded[c] for c in range(5))
    samples = []
    for step_index in range(STEPS):
        fields, moduli_map = advance(fields, moduli_map)
        moduli_map = [inner(m) for m in moduli_map]
        off = HALO - 2 * (step_index + 1)
        total = fields[2] + fields[3]
        tile = total[off:off + rows, off:off + cols]
        flat = tile.reshape(1, -1)
        samples.append(jnp.sum(jnp.where(hit, flat, jnp.float32(0.0)), axis=1))
        moduli_map = jnp.stack(moduli_map)
    next_state = jnp.stack(fields)[None]
    recorded = jnp.stack(samples, axis=1)[None]
    column = lax.broadcasted_iota(jnp.int32, hist_wide.shape, hist_wide.ndim - 1)
    trace_wide = jnp.pad(recorded[0], ((0, 0), (hist_count, 0)))
    spread = jnp.where(column >= hist_count, trace_wide[None], hist_wide)
    inner_waves = lax.all_to_all(spread, "hoop", 0, 0, tiled=True).reshape(
        (-1,) + spread.shape[2:]
    )
    waveforms = a2a_gather(inner_waves, "axial", lax.axis_size("axial"))
    partial_value = image(receivers[0], waveforms, delays[0])
    parts = lax.all_gather(partial_value.reshape(-1), "act").reshape((-1,) + partial_value.shape)
    summed = parts[0]
    for a in range(1, parts.shape[0]):
        summed = summed + parts[a]
    damage_map = summed * summed / (receivers.shape[1] * lax.axis_size("act"))
    return (next_state, recorded, damage_map)


def solution(mesh):
    return jax.shard_map(
        per_device,
        mesh=mesh,
        in_specs=(
            P("act", None, "axial", "hoop"),
            P("axial", "hoop"),
            P(),
            P(("axial", "hoop")),
            P("act", ("axial", "hoop"), None),
            P("act", None),
            P("act", None, "axial", "hoop"),
        ),
        out_specs=(
            P("act", None, "axial", "hoop"),
            P("act", ("axial", "hoop"), None),
            P("axial", "hoop"),
        ),
        check_vma=False,
    )
```
